256 devices in a mesh: tiles: 64 (over z, x, core), views: 4 (over y).
Axes of the slice: x: 4, y: 4, z: 8, core: 2. Of those that a mesh axis runs over, the one named last changes fastest.
Arguments:
- gaussians: float32 [59, 131072], P(None, 'tiles')
- moment_one: float32 [59, 131072], P(None, 'tiles'), may hold values from -3 to 3
- moment_two: float32 [59, 131072], P(None, 'tiles'), may hold values from 0.01 to 1
- learn_rates: float32 [59], replicated, may hold values from 0.002 to 0.05
- cameras: float32 [16, 12], replicated, as said below
- camera_ids: int32 [4], P('views'), may hold values from 0 to 15
- list_owner: int32 [4, 64, 1024, 1], P('views', 'tiles'), may hold values from 0 to 63; in each aligned block of 1024 rows (0 to 1023, 1024 to 2047, ..., all dimensions but the last counted through in order) at most 32 rows name the same one
- list_index: int32 [4, 64, 1024], P('views', 'tiles'), may hold values from 0 to 2047
- list_length: int32 [4, 64], P('views', 'tiles'), may hold values from 1 to 1024, 32768 in all within a row
- targets: bfloat16 [4, 64, 3, 1024], P('views', 'tiles'), may hold values from 0 to 1
- background: float32 [3], replicated, may hold values from 0.1 to 0.9
Outputs:
- rendered: bfloat16 [4, 64, 3, 1024], P('views', 'tiles')
- new_gaussians: float32 [59, 131072], P(None, 'tiles')
- new_moment_one: float32 [59, 131072], P(None, 'tiles')
- new_moment_two: float32 [59, 131072], P(None, 'tiles')
The draws below stay inside these ranges and needn't reach their ends.
Inputs may be any that keep to these rules, and one draw needn't show every extreme that they name: `list_owner`: in the list of one device (one camera slot, one tile) no owner is named by more than 32 entries, and some device's list reaches this bound. `cameras`: rotations are proper, and every Gaussian lies in front of every camera.
All inputs are finite; a program needn't handle non-finite values. No bound on the sum of `list_length` on one device may be relied on, other than what follows from the above.
Results may differ from the reference program's by a relative error of at most 0.001.
Values sent between devices are 32-bit elements; how exact they have to be, the bound alone decides.
No kernel may reach another device: no remote copies, remote signals or barrier semaphores. Data moves between devices by JAX's collectives and lax.ppermute only.
A program may use at most 192 MiB of HBM per device.

```python
import math
from functools import partial
import jax
import jax.numpy as jnp
import numpy as np
from jax import lax

TILE_SIDE = 32
PIXELS = 1024
TILE_ROWS = 8
LIST = 1024
CAMERAS = 16
TILES_DEV = 1
G_DEV = 2048
TILES = 64
TILE_COLS = 8
GAUSSIANS = 131072
CAP = 32
N_TILES = 64
N_VIEWS = 4


focal_length = 400.0


def draw_gaussians(key, part):
    keys = jax.random.split(key, 8)
    ident = jnp.arange(GAUSSIANS)
    local = ident % G_DEV
    home = local % TILES
    levels = G_DEV // TILES
    level = (local // TILES).astype(jnp.float32)
    pixel_x = (home % TILE_COLS * TILE_SIDE).astype(jnp.float32) + jax.random.uniform(keys[0], (GAUSSIANS,), jnp.float32) * TILE_SIDE
    pixel_y = (home // TILE_COLS * TILE_SIDE).astype(jnp.float32) + jax.random.uniform(keys[1], (GAUSSIANS,), jnp.float32) * TILE_SIDE
    depth = 10.0 + 20.0 * (level + 0.5 * jax.random.uniform(keys[2], (GAUSSIANS,), jnp.float32)) / levels
    center_x = 0.5 * TILE_SIDE * TILE_COLS
    center_y = 0.5 * TILE_SIDE * TILE_ROWS
    means = jnp.stack([(pixel_x - center_x) * depth / focal_length, (pixel_y - center_y) * depth / focal_length, depth])
    spread = jax.random.uniform(keys[3], (3, GAUSSIANS), jnp.float32, 1.5, 8.0)
    log_scale = jnp.log(spread * depth[None, :] / focal_length)
    quat = jnp.concatenate([jax.random.uniform(keys[4], (1, GAUSSIANS), jnp.float32, 0.5, 1.5), jax.random.uniform(keys[5], (3, GAUSSIANS), jnp.float32, -1.0, 1.0)], axis=0)
    logit = jax.random.uniform(keys[6], (1, GAUSSIANS), jnp.float32, -5.0, -2.0)
    coeffs = 0.4 * jnp.clip(jax.random.normal(keys[7], (48, GAUSSIANS), jnp.float32), -3.0, 3.0)
    return jnp.concatenate([means, log_scale, quat, logit, coeffs], axis=0).astype(jnp.float32)


def draw_cameras(key, part):
    keys = jax.random.split(key, 2)
    angles = jax.random.uniform(keys[0], (3, CAMERAS), jnp.float32, -0.02, 0.02)
    shift = jax.random.uniform(keys[1], (3, CAMERAS), jnp.float32, -0.1, 0.1)
    cos_x, sin_x = (jnp.cos(angles[0]), jnp.sin(angles[0]))
    cos_y, sin_y = (jnp.cos(angles[1]), jnp.sin(angles[1]))
    cos_z, sin_z = (jnp.cos(angles[2]), jnp.sin(angles[2]))
    entries = [cos_z * cos_y, cos_z * sin_y * sin_x - sin_z * cos_x, cos_z * sin_y * cos_x + sin_z * sin_x, sin_z * cos_y, sin_z * sin_y * sin_x + cos_z * cos_x, sin_z * sin_y * cos_x - cos_z * sin_x, -sin_y, cos_y * sin_x, cos_y * cos_x]
    table = jnp.concatenate([jnp.stack(entries), shift], axis=0)
    return table.T.astype(jnp.float32)


def draw_list_index(key, part):
    levels = G_DEV // TILES
    level = jnp.sort(jax.random.randint(key, (N_VIEWS, TILES, LIST), 0, levels), axis=-1)
    return (jnp.arange(TILES)[None, :, None] + TILES * level).astype(jnp.int32)


def plant(array, own_key, least, largest):
    longest = array.shape.index(max(array.shape))
    spots = []
    for shift in (0, 1):
        where = [jax.random.randint(jax.random.fold_in(own_key, axis), (), 0, length) for axis, length in enumerate(array.shape)]
        where[longest] = (where[longest] + shift) % array.shape[longest]
        spots.append(tuple(where))
    return array.at[spots[0]].set(least).at[spots[1]].set(largest)


def steps_of(own_key, shape, cuts, smallest, high):
    loudness = 1.0
    for axis_at, parts in cuts:
        draws = jax.random.uniform(jax.random.fold_in(jax.random.fold_in(own_key, 6), axis_at), (parts,), jnp.float32, smallest / len(cuts), high / len(cuts))
        loudness = loudness * jnp.repeat(jnp.exp(draws), shape[axis_at] // parts).reshape((-1,) + (1,) * (len(shape) - 1 - axis_at))
    return loudness


def length_profile(amount, total, reach, slope):
    weights = [(1 << 20) // math.isqrt(grade ** slope) + 1 for grade in range(2, amount + 1)]
    surplus, given = total - reach - (amount - 1), [1] * (amount - 1)
    while surplus > 0:
        candidates = [i for i in range(amount - 1) if given[i] < reach]
        pool, budget = sum([weights[i] for i in candidates]), surplus
        for i in candidates:
            addition = min(reach - given[i], max(1, budget * weights[i] // pool), surplus)
            given[i] = given[i] + addition
            surplus = surplus - addition
    return np.array([reach] + given)


def ragged_sizes(own_key, count, total, reach, skew):
    if count == 2:
        one = jax.random.randint(own_key, (), max(1, total - reach), min(reach, total - 1) + 1)
        return jnp.stack([one, total - one])
    tallies = jnp.asarray(length_profile(count, total, reach, skew), jnp.int32)
    pairs = (count - 1) // 2
    giver, sink = tallies[1:1 + 2 * pairs:2], tallies[2:2 + 2 * pairs:2]
    slack = jnp.minimum(giver - 1, reach - sink)
    passed = jax.random.randint(jax.random.fold_in(own_key, 1), (pairs,), 0, 1 << 20) % (slack + 1)
    tallies = tallies.at[1:1 + 2 * pairs:2].set(giver - passed).at[2:2 + 2 * pairs:2].set(sink + passed)
    return tallies[jax.random.permutation(jax.random.fold_in(own_key, 2), count)]


def assign_block(key, own, number, rows, count, top, most, skew):
    order = jax.random.permutation(key, count)
    packed, usual = load_shares(count, rows * top, most, skew, True), load_shares(count, rows * top, most, skew, False)
    places = jnp.arange(count)

    def named(lengths, offset_by):
        used = int((lengths > 0).sum())
        fixed = max(1, used // 4)
        shifted = fixed + (places - fixed + offset_by * (used - fixed)) % max(1, count - fixed)
        return jnp.zeros((count,), jnp.int32).at[order[jnp.where(places < fixed, places, shifted)]].set(jnp.asarray(lengths, jnp.int32))

    lengths = jnp.where(number % 4 == 0, named(packed, number // 4), named(usual, number - number // 4 - 1))
    mixed = jax.random.permutation(jax.random.fold_in(own, 3), count)
    giver, taker = mixed[0:count // 2 * 2:2], mixed[1:count // 2 * 2:2]
    room = jnp.minimum(lengths[giver] - 1, most - lengths[taker]) // 2
    room = jnp.where((giver == order[0]) | (taker == order[0]) | (lengths[taker] == 0), 0, jnp.maximum(room, 0))
    shifted = jax.random.randint(jax.random.fold_in(own, 4), (count // 2,), 0, 1 << 20) % (room + 1)
    lengths = lengths.at[giver].add(-shifted).at[taker].add(shifted)
    labels = jnp.searchsorted(jnp.cumsum(lengths), jnp.arange(rows * top), side="right").astype(jnp.int32)
    table = labels.reshape(top, rows).T
    table = table[jax.random.permutation(jax.random.fold_in(own, 1), rows)]
    offset_by = jax.random.randint(jax.random.fold_in(own, 2), (rows, 1), 0, top)
    return jnp.take_along_axis(table, (jnp.arange(top)[None, :] + offset_by) % top, axis=1)


def load_shares(amount, total, bound, slope, full):
    portions = [(1 << 20) // math.isqrt(rank ** slope) + 1 for rank in range(1, amount + 1)]
    largest = bound if full else min(bound, max(-(-total // amount), total * portions[0] // sum(portions)))
    least = 1 if total - largest >= amount - 1 else 0
    counts, rest = [largest] + [least] * (amount - 1), total - largest - least * (amount - 1)
    while rest > 0:
        candidates = [i for i in range(1, amount) if counts[i] < largest] or [i for i in range(1, amount) if counts[i] < bound]
        pool, budget = sum([portions[i] for i in candidates]), rest
        for i in candidates:
            addition = min(bound - counts[i], max(1, budget * portions[i] // pool), rest)
            counts[i] = counts[i] + addition
            rest = rest - addition
    return np.array(counts)


def noise(key, extent, deviation, limit, cuts=(), dtype=jnp.bfloat16):
    values = jax.random.normal(key, extent, jnp.float32) * deviation
    if len(cuts) > 0:
        values = steps_of(key, extent, cuts, -0.22, 0.18) * values
    return jnp.clip(values, min=-limit, max=limit).astype(dtype)


def setup_inputs(seed: int = 0) -> dict:
    key_of = jax.random.split(jax.random.key(seed), 12)
    gaussians = draw_gaussians(jax.random.fold_in(key_of[11], 71), 0)
    moment_one = noise(key_of[1], (59, GAUSSIANS), 0.5, 3.0, ((1, 64),), jnp.float32)
    moment_two = jnp.clip(jnp.exp(math.log(1.0) - 4.6051702 * jax.random.uniform(key_of[2], (59, GAUSSIANS), jnp.float32) ** steps_of(key_of[2], (59, GAUSSIANS), ((1, 64),), -0.2, 0.2)), 0.01, 1.0)
    learn_rates = jnp.clip(jnp.exp(jax.random.uniform(key_of[3], (59,), jnp.float32, math.log(0.002), math.log(0.05))), 0.002, 0.05)
    cameras = draw_cameras(jax.random.fold_in(key_of[11], 71), 0)
    camera_ids = plant(jax.random.randint(key_of[5], (N_VIEWS,), 0, CAMERAS), jax.random.fold_in(key_of[5], 1), 0, CAMERAS - 1).astype(jnp.int32)
    list_owner_keys = jax.random.split(jax.random.fold_in(key_of[6], 1), N_VIEWS * TILES * LIST // (TILES_DEV * LIST))
    list_owner_turns = jax.random.permutation(jax.random.fold_in(key_of[6], 3), N_VIEWS * TILES * LIST // (TILES_DEV * LIST))
    list_owner = jax.vmap(lambda own, number: assign_block(jax.random.fold_in(key_of[6], 2), own, number, TILES_DEV * LIST, N_TILES, 1, CAP, 2))(list_owner_keys, list_owner_turns).reshape((N_VIEWS, TILES, LIST, 1))
    list_index = draw_list_index(jax.random.fold_in(key_of[11], 71), 0)
    list_length = jax.vmap(lambda own: ragged_sizes(own, TILES, TILES * LIST // 2, LIST, 2))(jax.random.split(key_of[8], N_VIEWS)).reshape((N_VIEWS, TILES)).astype(jnp.int32)
    targets = jnp.clip(1.0 * jax.random.uniform(key_of[9], (N_VIEWS, TILES, 3, PIXELS), jnp.float32) ** steps_of(key_of[9], (N_VIEWS, TILES, 3, PIXELS), ((0, 4), (1, 64)), -0.2, 0.2), 0.0, 1.0).astype(jnp.bfloat16)
    background = jnp.clip(jax.random.uniform(key_of[10], (3,), jnp.float32, 0.1, 0.9), 0.1, 0.9)
    return {"gaussians": gaussians, "moment_one": moment_one, "moment_two": moment_two, "learn_rates": learn_rates, "cameras": cameras, "camera_ids": camera_ids, "list_owner": list_owner, "list_index": list_index, "list_length": list_length, "targets": targets, "background": background}


focal_length = 400.0
precise = lax.Precision.HIGHEST

def sh_basis(direction):
    dir_x, dir_y, dir_z = (direction[0], direction[1], direction[2])
    sq_x, sq_y, sq_z = (dir_x * dir_x, dir_y * dir_y, dir_z * dir_z)
    terms = [0.28209479177387814 * jnp.ones_like(dir_x), -0.4886025119029199 * dir_y, 0.4886025119029199 * dir_z, -0.4886025119029199 * dir_x, 1.0925484305920792 * dir_x * dir_y, -1.0925484305920792 * dir_y * dir_z, 0.31539156525252005 * (2.0 * sq_z - sq_x - sq_y), -1.0925484305920792 * dir_x * dir_z, 0.5462742152960396 * (sq_x - sq_y), -0.5900435899266435 * dir_y * (3.0 * sq_x - sq_y), 2.890611442640554 * dir_x * dir_y * dir_z, -0.4570457994644658 * dir_y * (4.0 * sq_z - sq_x - sq_y), 0.3731763325901154 * dir_z * (2.0 * sq_z - 3.0 * sq_x - 3.0 * sq_y), -0.4570457994644658 * dir_x * (4.0 * sq_z - sq_x - sq_y), 1.445305721320277 * dir_z * (sq_x - sq_y), -0.5900435899266435 * dir_x * (sq_x - 3.0 * sq_y)]
    return jnp.stack(terms)

def quat_rotation(quat):
    length = jnp.sqrt(lax.optimization_barrier(jnp.sum(quat * quat, axis=0)))
    quat_w, quat_x, quat_y, quat_z = (quat[0] / length, quat[1] / length, quat[2] / length, quat[3] / length)
    rows = [[1.0 - 2.0 * (quat_y * quat_y + quat_z * quat_z), 2.0 * (quat_x * quat_y - quat_w * quat_z), 2.0 * (quat_x * quat_z + quat_w * quat_y)], [2.0 * (quat_x * quat_y + quat_w * quat_z), 1.0 - 2.0 * (quat_x * quat_x + quat_z * quat_z), 2.0 * (quat_y * quat_z - quat_w * quat_x)], [2.0 * (quat_x * quat_z - quat_w * quat_y), 2.0 * (quat_y * quat_z + quat_w * quat_x), 1.0 - 2.0 * (quat_x * quat_x + quat_y * quat_y)]]
    return jnp.stack([jnp.stack(entries) for entries in rows])

def project(params, camera, center_x, center_y):
    means = params[0:3]
    rotate = camera[0:9].reshape(3, 3)
    shift = camera[9:12]
    view_pos = jnp.dot(rotate, means, precision=precise) + shift[:, None]
    inv_depth = 1.0 / view_pos[2]
    image_x = focal_length * view_pos[0] * inv_depth + center_x
    image_y = focal_length * view_pos[1] * inv_depth + center_y
    scales = jnp.exp(params[3:6])
    local_axes = quat_rotation(params[6:10]) * scales[None, :, :]
    world_axes = jnp.einsum('ik,kjg->ijg', rotate, local_axes, precision=precise)
    proj_x = focal_length * inv_depth * world_axes[0] - focal_length * view_pos[0] * inv_depth * inv_depth * world_axes[2]
    proj_y = focal_length * inv_depth * world_axes[1] - focal_length * view_pos[1] * inv_depth * inv_depth * world_axes[2]
    cov_xx = lax.optimization_barrier(jnp.sum(proj_x * proj_x, axis=0)) + 0.3
    cov_xy = lax.optimization_barrier(jnp.sum(proj_x * proj_y, axis=0))
    cov_yy = lax.optimization_barrier(jnp.sum(proj_y * proj_y, axis=0)) + 0.3
    determ = cov_xx * cov_yy - cov_xy * cov_xy
    opacity = 0.99 * jax.nn.sigmoid(params[10])
    center = -jnp.dot(rotate.T, shift, precision=precise)
    offset = means - center[:, None]
    direction = offset / jnp.sqrt(lax.optimization_barrier(jnp.sum(offset * offset, axis=0)))
    basis = sh_basis(direction)
    coeffs = params[11:59].reshape(16, 3, -1)
    colors = 0.5 + lax.optimization_barrier(jnp.sum(basis[:, None, :] * coeffs, axis=0))
    head = jnp.stack([image_x, image_y, cov_yy / determ, -cov_xy / determ, cov_xx / determ, opacity])
    return jnp.concatenate([head, colors], axis=0)

def pixel_grid(tile, tile_cols):
    offsets = jnp.arange(PIXELS)
    pixel_x = (tile % tile_cols * TILE_SIDE + offsets % TILE_SIDE).astype(jnp.float32) + 0.5
    pixel_y = (tile // tile_cols * TILE_SIDE + offsets // TILE_SIDE).astype(jnp.float32) + 0.5
    return (pixel_x, pixel_y)

def composite(entry, count, pixel_x, pixel_y, target, background):
    live = (jnp.arange(LIST) < count)[None, :]
    delta_x = pixel_x[:, None] - entry[0][None, :]
    delta_y = pixel_y[:, None] - entry[1][None, :]
    power = -0.5 * (entry[2] * delta_x * delta_x + 2.0 * entry[3] * delta_x * delta_y + entry[4] * delta_y * delta_y)
    falloff = jnp.exp(power)
    alpha = jnp.where(live, entry[5][None, :] * falloff, 0.0)
    log_keep = jnp.log1p(-alpha)
    trans = jnp.exp(jnp.cumsum(log_keep, axis=1) - log_keep)
    weight = trans * alpha
    image = jnp.dot(entry[6:9], weight.T, precision=precise) + jnp.exp(lax.optimization_barrier(jnp.sum(log_keep, axis=1)))[None, :] * background[:, None]
    resid = image - target
    along = jnp.dot(resid.T, entry[6:9], precision=precise)
    running = jnp.cumsum(weight * along, axis=1)
    dot_total = lax.optimization_barrier(jnp.sum(image * resid, axis=0))
    d_alpha = jnp.where(live, trans * along - (dot_total[:, None] - running) / (1.0 - alpha), 0.0)
    d_power = d_alpha * alpha
    sum_x = lax.optimization_barrier(jnp.sum(d_power * delta_x, axis=0))
    sum_y = lax.optimization_barrier(jnp.sum(d_power * delta_y, axis=0))
    head = jnp.stack([entry[2] * sum_x + entry[3] * sum_y, entry[3] * sum_x + entry[4] * sum_y, -0.5 * lax.optimization_barrier(jnp.sum(d_power * delta_x * delta_x, axis=0)), -lax.optimization_barrier(jnp.sum(d_power * delta_x * delta_y, axis=0)), -0.5 * lax.optimization_barrier(jnp.sum(d_power * delta_y * delta_y, axis=0)), lax.optimization_barrier(jnp.sum(d_alpha * falloff, axis=0))])
    color_grad = jnp.dot(resid, weight, precision=precise)
    return (image, jnp.concatenate([head, color_grad], axis=0))

def reference(gaussians, moment_one, moment_two, learn_rates, cameras, camera_ids, list_owner, list_index, list_length, targets, background):
    center_x = 0.5 * TILE_SIDE * TILE_COLS
    center_y = 0.5 * TILE_SIDE * TILE_ROWS
    grads = jnp.zeros(gaussians.shape, jnp.float32)
    images_all = []
    for view in range(N_VIEWS):
        camera = cameras[camera_ids[view]]
        attrs, pullback = jax.vjp(partial(project, camera=camera, center_x=center_x, center_y=center_y), gaussians)

        def per_tile(tile):
            ident = list_owner[view, tile, :, 0] * G_DEV + list_index[view, tile]
            entry = attrs[:, ident]
            pixel_x, pixel_y = pixel_grid(tile, TILE_COLS)
            image, entry_grads = composite(entry, list_length[view, tile], pixel_x, pixel_y, targets[view, tile].astype(jnp.float32), background)
            return (image, entry_grads, ident)
        images, tile_grads, idents = lax.map(per_tile, jnp.arange(TILES))
        flat = jnp.moveaxis(tile_grads, 1, 0).reshape(9, -1)
        attr_grad = jnp.zeros((9, GAUSSIANS), jnp.float32).at[:, idents.reshape(-1)].add(flat)
        grads = grads + pullback(attr_grad)[0]
        images_all.append(images.astype(jnp.bfloat16))
    first_new = 0.9 * moment_one + 0.1 * grads
    second_new = 0.999 * moment_two + 0.001 * grads * grads
    new_values = gaussians - learn_rates[:, None] * first_new / (jnp.sqrt(second_new) + 1e-08)
    return (jnp.stack(images_all), new_values, first_new, second_new)
```

```python
from functools import partial

import jax
import jax.numpy as jnp
from jax import lax
from jax.sharding import PartitionSpec as P

TILE_SIDE = 32
PIXELS = 1024
TILE_ROWS = 8
LIST = 1024
BLOCK = 128


focal_length = 400.0
precise = lax.Precision.HIGHEST
decay_one = 0.9
decay_two = 0.999
adam_epsilon = 1e-08


def sh_basis(direction):
    dir_x, dir_y, dir_z = (direction[0], direction[1], direction[2])
    sq_x, sq_y, sq_z = (dir_x * dir_x, dir_y * dir_y, dir_z * dir_z)
    terms = [
        0.28209479177387814 * jnp.ones_like(dir_x),
        -0.4886025119029199 * dir_y,
        0.4886025119029199 * dir_z,
        -0.4886025119029199 * dir_x,
        1.0925484305920792 * dir_x * dir_y,
        -1.0925484305920792 * dir_y * dir_z,
        0.31539156525252005 * (2.0 * sq_z - sq_x - sq_y),
        -1.0925484305920792 * dir_x * dir_z,
        0.5462742152960396 * (sq_x - sq_y),
        -0.5900435899266435 * dir_y * (3.0 * sq_x - sq_y),
        2.890611442640554 * dir_x * dir_y * dir_z,
        -0.4570457994644658 * dir_y * (4.0 * sq_z - sq_x - sq_y),
        0.3731763325901154 * dir_z * (2.0 * sq_z - 3.0 * sq_x - 3.0 * sq_y),
        -0.4570457994644658 * dir_x * (4.0 * sq_z - sq_x - sq_y),
        1.445305721320277 * dir_z * (sq_x - sq_y),
        -0.5900435899266435 * dir_x * (sq_x - 3.0 * sq_y),
    ]
    return jnp.stack(terms)


def quat_rotation(quat):
    length = jnp.sqrt(jnp.sum(quat * quat, axis=0))
    quat_w, quat_x, quat_y, quat_z = (
        quat[0] / length,
        quat[1] / length,
        quat[2] / length,
        quat[3] / length,
    )
    rows = [
        [
            1.0 - 2.0 * (quat_y * quat_y + quat_z * quat_z),
            2.0 * (quat_x * quat_y - quat_w * quat_z),
            2.0 * (quat_x * quat_z + quat_w * quat_y),
        ],
        [
            2.0 * (quat_x * quat_y + quat_w * quat_z),
            1.0 - 2.0 * (quat_x * quat_x + quat_z * quat_z),
            2.0 * (quat_y * quat_z - quat_w * quat_x),
        ],
        [
            2.0 * (quat_x * quat_z - quat_w * quat_y),
            2.0 * (quat_y * quat_z + quat_w * quat_x),
            1.0 - 2.0 * (quat_x * quat_x + quat_y * quat_y),
        ],
    ]
    return jnp.stack([jnp.stack(entries) for entries in rows])


def project(params, camera, center_x, center_y):
    means = params[0:3]
    rotate = camera[0:9].reshape(3, 3)
    shift = camera[9:12]
    view_pos = jnp.dot(rotate, means, precision=precise) + shift[:, None]
    inv_depth = 1.0 / view_pos[2]
    image_x = focal_length * view_pos[0] * inv_depth + center_x
    image_y = focal_length * view_pos[1] * inv_depth + center_y
    scales = jnp.exp(params[3:6])
    local_axes = quat_rotation(params[6:10]) * scales[None, :, :]
    world_axes = jnp.einsum("ik,kjg->ijg", rotate, local_axes, precision=precise)
    proj_x = (
        focal_length * inv_depth * world_axes[0]
        - focal_length * view_pos[0] * inv_depth * inv_depth * world_axes[2]
    )
    proj_y = (
        focal_length * inv_depth * world_axes[1]
        - focal_length * view_pos[1] * inv_depth * inv_depth * world_axes[2]
    )
    cov_xx = jnp.sum(proj_x * proj_x, axis=0) + 0.3
    cov_xy = jnp.sum(proj_x * proj_y, axis=0)
    cov_yy = jnp.sum(proj_y * proj_y, axis=0) + 0.3
    determ = cov_xx * cov_yy - cov_xy * cov_xy
    opacity = 0.99 * jax.nn.sigmoid(params[10])
    center = -jnp.dot(rotate.T, shift, precision=precise)
    offset = means - center[:, None]
    direction = offset / jnp.sqrt(jnp.sum(offset * offset, axis=0))
    basis = sh_basis(direction)
    coeffs = params[11:59].reshape(16, 3, -1)
    colors = 0.5 + jnp.sum(basis[:, None, :] * coeffs, axis=0)
    head = jnp.stack(
        [image_x, image_y, cov_yy / determ, -cov_xy / determ, cov_xx / determ, opacity]
    )
    return jnp.concatenate([head, colors], axis=0)


def pixel_grid(tile, tile_cols):
    offsets = jnp.arange(PIXELS)
    pixel_x = (tile % tile_cols * TILE_SIDE + offsets % TILE_SIDE).astype(jnp.float32) + 0.5
    pixel_y = (tile // tile_cols * TILE_SIDE + offsets // TILE_SIDE).astype(jnp.float32) + 0.5
    return (pixel_x, pixel_y)


def block_terms(entry, count, pixel_x, pixel_y, index):
    start = index * BLOCK
    piece = lax.dynamic_slice_in_dim(entry, start, BLOCK, 1)
    live = (start + jnp.arange(BLOCK) < count)[None, :]
    delta_x = pixel_x[:, None] - piece[0][None, :]
    delta_y = pixel_y[:, None] - piece[1][None, :]
    power = -0.5 * (
        piece[2] * delta_x * delta_x
        + 2.0 * piece[3] * delta_x * delta_y
        + piece[4] * delta_y * delta_y
    )
    falloff = jnp.exp(power)
    alpha = jnp.where(live, piece[5][None, :] * falloff, 0.0)
    log_keep = jnp.log1p(-alpha)
    return (start, piece, live, delta_x, delta_y, falloff, alpha, log_keep)


def tile_pass(entry, count, pixel_x, pixel_y, target, background):
    blocks = (count + BLOCK - 1) // BLOCK

    def forward(index, carry):
        color, log_total = carry
        start, piece, live, delta_x, delta_y, falloff, alpha, log_keep = block_terms(
            entry, count, pixel_x, pixel_y, index
        )
        weight = jnp.exp(log_total[:, None] + jnp.cumsum(log_keep, axis=1) - log_keep) * alpha
        color = color + lax.dot_general(
            piece[6:9], weight, (((1,), (1,)), ((), ())), precision=precise
        )
        return (color, log_total + jnp.sum(log_keep, axis=1))

    zeros_pix = jnp.zeros((PIXELS,), jnp.float32)
    color, log_total = lax.fori_loop(
        0, blocks, forward, (jnp.zeros((3, PIXELS), jnp.float32), zeros_pix)
    )
    image = color + jnp.exp(log_total)[None, :] * background[:, None]
    resid = image - target
    dot_total = jnp.sum(image * resid, axis=0)

    def backward(index, carry):
        grads, log_before, prefix = carry
        start, piece, live, delta_x, delta_y, falloff, alpha, log_keep = block_terms(
            entry, count, pixel_x, pixel_y, index
        )
        trans = jnp.exp(log_before[:, None] + jnp.cumsum(log_keep, axis=1) - log_keep)
        weight = trans * alpha
        along = lax.dot_general(resid, piece[6:9], (((0,), (0,)), ((), ())), precision=precise)
        running = prefix[:, None] + jnp.cumsum(weight * along, axis=1)
        d_alpha = jnp.where(
            live, trans * along - (dot_total[:, None] - running) / (1.0 - alpha), 0.0
        )
        d_power = d_alpha * alpha
        sum_x = jnp.sum(d_power * delta_x, axis=0)
        sum_y = jnp.sum(d_power * delta_y, axis=0)
        head = jnp.stack(
            [
                piece[2] * sum_x + piece[3] * sum_y,
                piece[3] * sum_x + piece[4] * sum_y,
                -0.5 * jnp.sum(d_power * delta_x * delta_x, axis=0),
                -jnp.sum(d_power * delta_x * delta_y, axis=0),
                -0.5 * jnp.sum(d_power * delta_y * delta_y, axis=0),
                jnp.sum(d_alpha * falloff, axis=0),
            ]
        )
        color_grad = jnp.dot(resid, weight, precision=precise)
        block_grad = jnp.concatenate([head, color_grad], axis=0)
        grads = lax.dynamic_update_slice_in_dim(grads, block_grad, start, 1)
        return (grads, log_before + jnp.sum(log_keep, axis=1), running[:, -1])

    start_grads = jnp.zeros((9, LIST), jnp.float32)
    grads, ignored, unused = lax.fori_loop(0, blocks, backward, (start_grads, zeros_pix, zeros_pix))
    return (image, grads)


def adam_step(values, first, second, grad, rates):
    first_new = decay_one * first + (1.0 - decay_one) * grad
    second_new = decay_two * second + (1.0 - decay_two) * grad * grad
    return (
        values - rates[:, None] * first_new / (jnp.sqrt(second_new) + adam_epsilon),
        first_new,
        second_new,
    )


def body(
    gaussians,
    moment_one,
    moment_two,
    learn_rates,
    cameras,
    camera_ids,
    list_owner,
    list_index,
    list_length,
    targets,
    background,
):
    peers = lax.axis_size("tiles")
    tiles_here = list_index.shape[1]
    entries = tiles_here * LIST
    owned = gaussians.shape[1]
    capacity = 2 * entries // peers
    tile_cols = tiles_here * peers // TILE_ROWS
    center_x = 0.5 * TILE_SIDE * tile_cols
    center_y = 0.5 * TILE_SIDE * TILE_ROWS
    view_cameras = cameras[camera_ids]
    camera = view_cameras[lax.axis_index("views")]
    attrs = project(gaussians, camera, center_x, center_y)
    owner_flat = list_owner.reshape(-1)
    index_flat = list_index.reshape(-1)
    one_hot = (owner_flat[:, None] == jnp.arange(peers)[None, :]).astype(jnp.int32)
    rank = jnp.sum((jnp.cumsum(one_hot, axis=0) - 1) * one_hot, axis=1)
    slot = owner_flat * capacity + rank
    asked_for = (
        jnp.zeros((peers * capacity,), jnp.int32)
        .at[slot]
        .set(index_flat, unique_indices=True)
        .reshape(peers, capacity)
    )
    asked = lax.all_to_all(asked_for, "tiles", split_axis=0, concat_axis=0, tiled=True)
    served = jnp.take(attrs, asked, axis=1)
    returned = lax.all_to_all(served, "tiles", split_axis=1, concat_axis=1, tiled=True)
    entry_attrs = returned.reshape(9, peers * capacity)[:, slot].reshape(9, tiles_here, LIST)
    first_tile = lax.axis_index("tiles") * tiles_here

    def render(item):
        local_tile, entry, count, target = item
        pixel_x, pixel_y = pixel_grid(first_tile + local_tile, tile_cols)
        return tile_pass(entry, count, pixel_x, pixel_y, target.astype(jnp.float32), background)

    images, tile_grads = lax.map(
        render,
        (jnp.arange(tiles_here), jnp.moveaxis(entry_attrs, 1, 0), list_length[0], targets[0]),
    )
    flat_grads = jnp.moveaxis(tile_grads, 0, 1).reshape(9, entries)
    grad_send = (
        jnp.zeros((9, peers * capacity), jnp.float32)
        .at[:, slot]
        .set(flat_grads, unique_indices=True)
        .reshape(9, peers, capacity)
    )
    grad_back = lax.all_to_all(grad_send, "tiles", split_axis=1, concat_axis=1, tiled=True)
    attr_grad = (
        jnp.zeros((9, owned), jnp.float32)
        .at[:, asked.reshape(-1)]
        .add(grad_back.reshape(9, peers * capacity))
    )
    view_grads = lax.all_gather(attr_grad, "views", axis=0, tiled=False)

    def pull(view_camera, grad):
        ignored, pullback = jax.vjp(
            partial(project, camera=view_camera, center_x=center_x, center_y=center_y),
            gaussians,
        )
        return pullback(grad)[0]

    total = jnp.sum(jax.vmap(pull)(view_cameras, view_grads), axis=0)
    new_values, first_new, second_new = adam_step(
        gaussians, moment_one, moment_two, total, learn_rates
    )
    return (images[None].astype(jnp.bfloat16), new_values, first_new, second_new)


def solution(mesh):
    return jax.shard_map(
        body,
        mesh=mesh,
        in_specs=(
            P(None, "tiles"),
            P(None, "tiles"),
            P(None, "tiles"),
            P(),
            P(),
            P(),
            P("views", "tiles", None, None),
            P("views", "tiles", None),
            P("views", "tiles"),
            P("views", "tiles", None, None),
            P(),
        ),
        out_specs=(
            P("views", "tiles", None, None),
            P(None, "tiles"),
            P(None, "tiles"),
            P(None, "tiles"),
        ),
        check_vma=False,
    )
```

```python
from functools import partial

import jax
import jax.numpy as jnp
from jax import lax
from jax.sharding import PartitionSpec as P

TILE_SIDE = 32
PIXELS = 1024
TILE_ROWS = 8
LIST = 1024
BLOCK = 128


focal_length = 400.0
precise = lax.Precision.HIGHEST
decay_one = 0.9
decay_two = 0.999
adam_epsilon = 1e-08


def sh_basis(direction):
    dir_x, dir_y, dir_z = (direction[0], direction[1], direction[2])
    sq_x, sq_y, sq_z = (dir_x * dir_x, dir_y * dir_y, dir_z * dir_z)
    terms = [
        0.28209479177387814 * jnp.ones_like(dir_x),
        -0.4886025119029199 * dir_y,
        0.4886025119029199 * dir_z,
        -0.4886025119029199 * dir_x,
        1.0925484305920792 * dir_x * dir_y,
        -1.0925484305920792 * dir_y * dir_z,
        0.31539156525252005 * (2.0 * sq_z - sq_x - sq_y),
        -1.0925484305920792 * dir_x * dir_z,
        0.5462742152960396 * (sq_x - sq_y),
        -0.5900435899266435 * dir_y * (3.0 * sq_x - sq_y),
        2.890611442640554 * dir_x * dir_y * dir_z,
        -0.4570457994644658 * dir_y * (4.0 * sq_z - sq_x - sq_y),
        0.3731763325901154 * dir_z * (2.0 * sq_z - 3.0 * sq_x - 3.0 * sq_y),
        -0.4570457994644658 * dir_x * (4.0 * sq_z - sq_x - sq_y),
        1.445305721320277 * dir_z * (sq_x - sq_y),
        -0.5900435899266435 * dir_x * (sq_x - 3.0 * sq_y),
    ]
    return jnp.stack(terms)


def quat_rotation(quat):
    length = jnp.sqrt(jnp.sum(quat * quat, axis=0))
    quat_w, quat_x, quat_y, quat_z = (
        quat[0] / length,
        quat[1] / length,
        quat[2] / length,
        quat[3] / length,
    )
    rows = [
        [
            1.0 - 2.0 * (quat_y * quat_y + quat_z * quat_z),
            2.0 * (quat_x * quat_y - quat_w * quat_z),
            2.0 * (quat_x * quat_z + quat_w * quat_y),
        ],
        [
            2.0 * (quat_x * quat_y + quat_w * quat_z),
            1.0 - 2.0 * (quat_x * quat_x + quat_z * quat_z),
            2.0 * (quat_y * quat_z - quat_w * quat_x),
        ],
        [
            2.0 * (quat_x * quat_z - quat_w * quat_y),
            2.0 * (quat_y * quat_z + quat_w * quat_x),
            1.0 - 2.0 * (quat_x * quat_x + quat_y * quat_y),
        ],
    ]
    return jnp.stack([jnp.stack(entries) for entries in rows])


def project(params, camera, center_x, center_y):
    means = params[0:3]
    rotate = camera[0:9].reshape(3, 3)
    shift = camera[9:12]
    view_pos = jnp.dot(rotate, means, precision=precise) + shift[:, None]
    inv_depth = 1.0 / view_pos[2]
    image_x = focal_length * view_pos[0] * inv_depth + center_x
    image_y = focal_length * view_pos[1] * inv_depth + center_y
    scales = jnp.exp(params[3:6])
    local_axes = quat_rotation(params[6:10]) * scales[None, :, :]
    world_axes = jnp.einsum("ik,kjg->ijg", rotate, local_axes, precision=precise)
    proj_x = (
        focal_length * inv_depth * world_axes[0]
        - focal_length * view_pos[0] * inv_depth * inv_depth * world_axes[2]
    )
    proj_y = (
        focal_length * inv_depth * world_axes[1]
        - focal_length * view_pos[1] * inv_depth * inv_depth * world_axes[2]
    )
    cov_xx = jnp.sum(proj_x * proj_x, axis=0) + 0.3
    cov_xy = jnp.sum(proj_x * proj_y, axis=0)
    cov_yy = jnp.sum(proj_y * proj_y, axis=0) + 0.3
    determ = cov_xx * cov_yy - cov_xy * cov_xy
    opacity = 0.99 * jax.nn.sigmoid(params[10])
    center = -jnp.dot(rotate.T, shift, precision=precise)
    offset = means - center[:, None]
    direction = offset / jnp.sqrt(jnp.sum(offset * offset, axis=0))
    basis = sh_basis(direction)
    coeffs = params[11:59].reshape(16, 3, -1)
    colors = 0.5 + jnp.sum(basis[:, None, :] * coeffs, axis=0)
    head = jnp.stack(
        [image_x, image_y, cov_yy / determ, -cov_xy / determ, cov_xx / determ, opacity]
    )
    return jnp.concatenate([head, colors], axis=0)


def pixel_grid(tile, tile_cols):
    offsets = jnp.arange(PIXELS)
    pixel_x = (tile % tile_cols * TILE_SIDE + offsets % TILE_SIDE).astype(jnp.float32) + 0.5
    pixel_y = (tile // tile_cols * TILE_SIDE + offsets // TILE_SIDE).astype(jnp.float32) + 0.5
    return (pixel_x, pixel_y)


def block_terms(entry, count, pixel_x, pixel_y, index):
    start = index * BLOCK
    piece = lax.dynamic_slice_in_dim(entry, start, BLOCK, 1)
    live = (start + jnp.arange(BLOCK) < count)[None, :]
    delta_x = pixel_x[:, None] - piece[0][None, :]
    delta_y = pixel_y[:, None] - piece[1][None, :]
    power = -0.5 * (
        piece[2] * delta_x * delta_x
        + 2.0 * piece[3] * delta_x * delta_y
        + piece[4] * delta_y * delta_y
    )
    falloff = jnp.exp(power)
    alpha = jnp.where(live, piece[5][None, :] * falloff, 0.0)
    log_keep = jnp.log1p(-alpha)
    return (start, piece, live, delta_x, delta_y, falloff, alpha, log_keep)


def tile_pass(entry, count, pixel_x, pixel_y, target, background):
    blocks = (count + BLOCK - 1) // BLOCK

    def forward(index, carry):
        color, log_total = carry
        start, piece, live, delta_x, delta_y, falloff, alpha, log_keep = block_terms(
            entry, count, pixel_x, pixel_y, index
        )
        weight = jnp.exp(log_total[:, None] + jnp.cumsum(log_keep, axis=1) - log_keep) * alpha
        color = color + lax.dot_general(
            piece[6:9], weight, (((1,), (1,)), ((), ())), precision=precise
        )
        return (color, log_total + jnp.sum(log_keep, axis=1))

    zeros_pix = jnp.zeros((PIXELS,), jnp.float32)
    color, log_total = lax.fori_loop(
        0, blocks, forward, (jnp.zeros((3, PIXELS), jnp.float32), zeros_pix)
    )
    image = color + jnp.exp(log_total)[None, :] * background[:, None]
    resid = image - target
    dot_total = jnp.sum(image * resid, axis=0)

    def backward(index, carry):
        grads, log_before, prefix = carry
        start, piece, live, delta_x, delta_y, falloff, alpha, log_keep = block_terms(
            entry, count, pixel_x, pixel_y, index
        )
        trans = jnp.exp(log_before[:, None] + jnp.cumsum(log_keep, axis=1) - log_keep)
        weight = trans * alpha
        along = lax.dot_general(resid, piece[6:9], (((0,), (0,)), ((), ())), precision=precise)
        running = prefix[:, None] + jnp.cumsum(weight * along, axis=1)
        d_alpha = jnp.where(
            live, trans * along - (dot_total[:, None] - running) / (1.0 - alpha), 0.0
        )
        d_power = d_alpha * alpha
        sum_x = jnp.sum(d_power * delta_x, axis=0)
        sum_y = jnp.sum(d_power * delta_y, axis=0)
        head = jnp.stack(
            [
                piece[2] * sum_x + piece[3] * sum_y,
                piece[3] * sum_x + piece[4] * sum_y,
                -0.5 * jnp.sum(d_power * delta_x * delta_x, axis=0),
                -jnp.sum(d_power * delta_x * delta_y, axis=0),
                -0.5 * jnp.sum(d_power * delta_y * delta_y, axis=0),
                jnp.sum(d_alpha * falloff, axis=0),
            ]
        )
        color_grad = jnp.dot(resid, weight, precision=precise)
        block_grad = jnp.concatenate([head, color_grad], axis=0)
        grads = lax.dynamic_update_slice_in_dim(grads, block_grad, start, 1)
        return (grads, log_before + jnp.sum(log_keep, axis=1), running[:, -1])

    start_grads = jnp.zeros((9, LIST), jnp.float32)
    grads, ignored, unused = lax.fori_loop(0, blocks, backward, (start_grads, zeros_pix, zeros_pix))
    return (image, grads)


def adam_step(values, first, second, grad, rates):
    first_new = decay_one * first + (1.0 - decay_one) * grad
    second_new = decay_two * second + (1.0 - decay_two) * grad * grad
    return (
        values - rates[:, None] * first_new / (jnp.sqrt(second_new) + adam_epsilon),
        first_new,
        second_new,
    )


def body(
    gaussians,
    moment_one,
    moment_two,
    learn_rates,
    cameras,
    camera_ids,
    list_owner,
    list_index,
    list_length,
    targets,
    background,
):
    peers = lax.axis_size("tiles")
    tiles_here = list_index.shape[1]
    entries = tiles_here * LIST
    owned = gaussians.shape[1]
    capacity = 2 * entries // peers
    tile_cols = tiles_here * peers // TILE_ROWS
    center_x = 0.5 * TILE_SIDE * tile_cols
    center_y = 0.5 * TILE_SIDE * TILE_ROWS
    camera = cameras[camera_ids[0]]
    attrs = project(gaussians, camera, center_x, center_y)
    owner_flat = list_owner.reshape(-1)
    index_flat = list_index.reshape(-1)
    earlier = jnp.arange(entries)[None, :] < jnp.arange(entries)[:, None]
    same = owner_flat[:, None] == owner_flat[None, :]
    rank = jnp.sum((same & earlier).astype(jnp.int32), axis=1)
    slot = owner_flat * capacity + rank
    asked_for = (
        jnp.zeros((peers * capacity,), jnp.int32)
        .at[slot]
        .set(index_flat, unique_indices=True)
        .reshape(peers, capacity)
    )
    asked = lax.all_to_all(asked_for, "tiles", split_axis=0, concat_axis=0, tiled=True)
    served = jnp.take(attrs, asked, axis=1)
    returned = lax.all_to_all(served, "tiles", split_axis=1, concat_axis=1, tiled=True)
    entry_attrs = returned.reshape(9, peers * capacity)[:, slot].reshape(9, tiles_here, LIST)
    first_tile = lax.axis_index("tiles") * tiles_here

    def render(item):
        local_tile, entry, count, target = item
        pixel_x, pixel_y = pixel_grid(first_tile + local_tile, tile_cols)
        return tile_pass(entry, count, pixel_x, pixel_y, target.astype(jnp.float32), background)

    images, tile_grads = lax.map(
        render,
        (jnp.arange(tiles_here), jnp.moveaxis(entry_attrs, 1, 0), list_length[0], targets[0]),
    )
    flat_grads = jnp.moveaxis(tile_grads, 0, 1).reshape(9, entries)
    grad_send = (
        jnp.zeros((9, peers * capacity), jnp.float32)
        .at[:, slot]
        .set(flat_grads, unique_indices=True)
        .reshape(9, peers, capacity)
    )
    grad_back = lax.all_to_all(grad_send, "tiles", split_axis=1, concat_axis=1, tiled=True)
    attr_grad = (
        jnp.zeros((9, owned), jnp.float32)
        .at[:, asked.reshape(-1)]
        .add(grad_back.reshape(9, peers * capacity))
    )
    payload = jnp.concatenate([attr_grad.reshape(-1), jnp.pad(camera, (0, 128 - 12))])
    gathered = lax.all_gather(payload.reshape(-1, 128), "views", axis=0, tiled=False)
    gathered = gathered.reshape(gathered.shape[0], -1)
    view_grads = gathered[:, : 9 * owned].reshape(-1, 9, owned)
    view_cameras = gathered[:, 9 * owned : 9 * owned + 12]

    def pull(view_camera, grad):
        ignored, pullback = jax.vjp(
            partial(project, camera=view_camera, center_x=center_x, center_y=center_y),
            gaussians,
        )
        return pullback(grad)[0]

    total = jnp.sum(jax.vmap(pull)(view_cameras, view_grads), axis=0)
    new_values, first_new, second_new = adam_step(
        gaussians, moment_one, moment_two, total, learn_rates
    )
    return (images[None].astype(jnp.bfloat16), new_values, first_new, second_new)


def solution(mesh):
    return jax.shard_map(
        body,
        mesh=mesh,
        in_specs=(
            P(None, "tiles"),
            P(None, "tiles"),
            P(None, "tiles"),
            P(),
            P(),
            P("views"),
            P("views", "tiles", None, None),
            P("views", "tiles", None),
            P("views", "tiles"),
            P("views", "tiles", None, None),
            P(),
        ),
        out_specs=(
            P("views", "tiles", None, None),
            P(None, "tiles"),
            P(None, "tiles"),
            P(None, "tiles"),
        ),
        check_vma=False,
    )
```

```python
from functools import partial

import jax
import jax.numpy as jnp
from jax import lax
from jax.experimental import pallas as pl
from jax.experimental.pallas import tpu as pltpu
from jax.sharding import PartitionSpec as P

TILE_SIDE = 32
PIXELS = 1024
TILE_ROWS = 8
LIST = 1024
BLOCK = 128
KB = 128
PC = 128


focal_length = 400.0
precise = lax.Precision.HIGHEST
decay_one = 0.9
decay_two = 0.999
adam_epsilon = 1e-08


def sh_basis(direction):
    dir_x, dir_y, dir_z = (direction[0], direction[1], direction[2])
    sq_x, sq_y, sq_z = (dir_x * dir_x, dir_y * dir_y, dir_z * dir_z)
    terms = [
        0.28209479177387814 * jnp.ones_like(dir_x),
        -0.4886025119029199 * dir_y,
        0.4886025119029199 * dir_z,
        -0.4886025119029199 * dir_x,
        1.0925484305920792 * dir_x * dir_y,
        -1.0925484305920792 * dir_y * dir_z,
        0.31539156525252005 * (2.0 * sq_z - sq_x - sq_y),
        -1.0925484305920792 * dir_x * dir_z,
        0.5462742152960396 * (sq_x - sq_y),
        -0.5900435899266435 * dir_y * (3.0 * sq_x - sq_y),
        2.890611442640554 * dir_x * dir_y * dir_z,
        -0.4570457994644658 * dir_y * (4.0 * sq_z - sq_x - sq_y),
        0.3731763325901154 * dir_z * (2.0 * sq_z - 3.0 * sq_x - 3.0 * sq_y),
        -0.4570457994644658 * dir_x * (4.0 * sq_z - sq_x - sq_y),
        1.445305721320277 * dir_z * (sq_x - sq_y),
        -0.5900435899266435 * dir_x * (sq_x - 3.0 * sq_y),
    ]
    return jnp.stack(terms)


def quat_rotation(quat):
    length = jnp.sqrt(jnp.sum(quat * quat, axis=0))
    quat_w, quat_x, quat_y, quat_z = (
        quat[0] / length,
        quat[1] / length,
        quat[2] / length,
        quat[3] / length,
    )
    rows = [
        [
            1.0 - 2.0 * (quat_y * quat_y + quat_z * quat_z),
            2.0 * (quat_x * quat_y - quat_w * quat_z),
            2.0 * (quat_x * quat_z + quat_w * quat_y),
        ],
        [
            2.0 * (quat_x * quat_y + quat_w * quat_z),
            1.0 - 2.0 * (quat_x * quat_x + quat_z * quat_z),
            2.0 * (quat_y * quat_z - quat_w * quat_x),
        ],
        [
            2.0 * (quat_x * quat_z - quat_w * quat_y),
            2.0 * (quat_y * quat_z + quat_w * quat_x),
            1.0 - 2.0 * (quat_x * quat_x + quat_y * quat_y),
        ],
    ]
    return jnp.stack([jnp.stack(entries) for entries in rows])


def project(params, camera, center_x, center_y):
    means = params[0:3]
    rotate = camera[0:9].reshape(3, 3)
    shift = camera[9:12]
    view_pos = jnp.dot(rotate, means, precision=precise) + shift[:, None]
    inv_depth = 1.0 / view_pos[2]
    image_x = focal_length * view_pos[0] * inv_depth + center_x
    image_y = focal_length * view_pos[1] * inv_depth + center_y
    scales = jnp.exp(params[3:6])
    local_axes = quat_rotation(params[6:10]) * scales[None, :, :]
    world_axes = jnp.einsum("ik,kjg->ijg", rotate, local_axes, precision=precise)
    proj_x = (
        focal_length * inv_depth * world_axes[0]
        - focal_length * view_pos[0] * inv_depth * inv_depth * world_axes[2]
    )
    proj_y = (
        focal_length * inv_depth * world_axes[1]
        - focal_length * view_pos[1] * inv_depth * inv_depth * world_axes[2]
    )
    cov_xx = jnp.sum(proj_x * proj_x, axis=0) + 0.3
    cov_xy = jnp.sum(proj_x * proj_y, axis=0)
    cov_yy = jnp.sum(proj_y * proj_y, axis=0) + 0.3
    determ = cov_xx * cov_yy - cov_xy * cov_xy
    opacity = 0.99 * jax.nn.sigmoid(params[10])
    center = -jnp.dot(rotate.T, shift, precision=precise)
    offset = means - center[:, None]
    direction = offset / jnp.sqrt(jnp.sum(offset * offset, axis=0))
    basis = sh_basis(direction)
    coeffs = params[11:59].reshape(16, 3, -1)
    colors = 0.5 + jnp.sum(basis[:, None, :] * coeffs, axis=0)
    head = jnp.stack(
        [image_x, image_y, cov_yy / determ, -cov_xy / determ, cov_xx / determ, opacity]
    )
    return jnp.concatenate([head, colors], axis=0)


def pixel_grid(tile, tile_cols):
    offsets = jnp.arange(PIXELS)
    pixel_x = (tile % tile_cols * TILE_SIDE + offsets % TILE_SIDE).astype(jnp.float32) + 0.5
    pixel_y = (tile // tile_cols * TILE_SIDE + offsets // TILE_SIDE).astype(jnp.float32) + 0.5
    return (pixel_x, pixel_y)


def block_terms(entry, count, pixel_x, pixel_y, index):
    start = index * BLOCK
    piece = lax.dynamic_slice_in_dim(entry, start, BLOCK, 1)
    live = (start + jnp.arange(BLOCK) < count)[None, :]
    delta_x = pixel_x[:, None] - piece[0][None, :]
    delta_y = pixel_y[:, None] - piece[1][None, :]
    power = -0.5 * (
        piece[2] * delta_x * delta_x
        + 2.0 * piece[3] * delta_x * delta_y
        + piece[4] * delta_y * delta_y
    )
    falloff = jnp.exp(power)
    alpha = jnp.where(live, piece[5][None, :] * falloff, 0.0)
    log_keep = jnp.log1p(-alpha)
    return (start, piece, live, delta_x, delta_y, falloff, alpha, log_keep)


def tile_pass(entry, count, pixel_x, pixel_y, target, background):
    blocks = (count + BLOCK - 1) // BLOCK

    def forward(index, carry):
        color, log_total = carry
        start, piece, live, delta_x, delta_y, falloff, alpha, log_keep = block_terms(
            entry, count, pixel_x, pixel_y, index
        )
        weight = jnp.exp(log_total[:, None] + jnp.cumsum(log_keep, axis=1) - log_keep) * alpha
        color = color + lax.dot_general(
            piece[6:9], weight, (((1,), (1,)), ((), ())), precision=precise
        )
        return (color, log_total + jnp.sum(log_keep, axis=1))

    zeros_pix = jnp.zeros((PIXELS,), jnp.float32)
    color, log_total = lax.fori_loop(
        0, blocks, forward, (jnp.zeros((3, PIXELS), jnp.float32), zeros_pix)
    )
    image = color + jnp.exp(log_total)[None, :] * background[:, None]
    resid = image - target
    dot_total = jnp.sum(image * resid, axis=0)

    def backward(index, carry):
        grads, log_before, prefix = carry
        start, piece, live, delta_x, delta_y, falloff, alpha, log_keep = block_terms(
            entry, count, pixel_x, pixel_y, index
        )
        trans = jnp.exp(log_before[:, None] + jnp.cumsum(log_keep, axis=1) - log_keep)
        weight = trans * alpha
        along = lax.dot_general(resid, piece[6:9], (((0,), (0,)), ((), ())), precision=precise)
        running = prefix[:, None] + jnp.cumsum(weight * along, axis=1)
        d_alpha = jnp.where(
            live, trans * along - (dot_total[:, None] - running) / (1.0 - alpha), 0.0
        )
        d_power = d_alpha * alpha
        sum_x = jnp.sum(d_power * delta_x, axis=0)
        sum_y = jnp.sum(d_power * delta_y, axis=0)
        head = jnp.stack(
            [
                piece[2] * sum_x + piece[3] * sum_y,
                piece[3] * sum_x + piece[4] * sum_y,
                -0.5 * jnp.sum(d_power * delta_x * delta_x, axis=0),
                -jnp.sum(d_power * delta_x * delta_y, axis=0),
                -0.5 * jnp.sum(d_power * delta_y * delta_y, axis=0),
                jnp.sum(d_alpha * falloff, axis=0),
            ]
        )
        color_grad = jnp.dot(resid, weight, precision=precise)
        block_grad = jnp.concatenate([head, color_grad], axis=0)
        grads = lax.dynamic_update_slice_in_dim(grads, block_grad, start, 1)
        return (grads, log_before + jnp.sum(log_keep, axis=1), running[:, -1])

    start_grads = jnp.zeros((9, LIST), jnp.float32)
    grads, ignored, unused = lax.fori_loop(0, blocks, backward, (start_grads, zeros_pix, zeros_pix))
    return (image, grads)


def render_kernel(counts_ref, tiles_ref, entry_ref, target_ref, bg_ref, image_ref, sums_ref, *, tile_cols):
    t = pl.program_id(0)
    count = counts_ref[t]
    tile = tiles_ref[t]
    blocks = (count + KB - 1) // KB
    sums_ref[...] = jnp.zeros(sums_ref.shape, jnp.float32)
    row = lax.broadcasted_iota(jnp.int32, (KB, KB), 0)
    col = lax.broadcasted_iota(jnp.int32, (KB, KB), 1)
    upper = (row <= col).astype(jnp.float32)
    lane = lax.broadcasted_iota(jnp.int32, (1, KB), 1)
    base_x = (tile % tile_cols) * TILE_SIDE
    base_y = (tile // tile_cols) * TILE_SIDE
    bg = bg_ref[...]

    def terms(index, pix_x, pix_y):
        start = pl.multiple_of(index * KB, KB)
        blk = entry_ref[:, pl.ds(start, KB)]
        live = (start + lane) < count
        delta_x = pix_x - blk[0:1]
        delta_y = pix_y - blk[1:2]
        power = -0.5 * (blk[2:3] * delta_x * delta_x + 2.0 * blk[3:4] * delta_x * delta_y + blk[4:5] * delta_y * delta_y)
        falloff = jnp.exp(power)
        alpha = jnp.where(live, blk[5:6] * falloff, 0.0)
        log_keep = jnp.log1p(-alpha)
        cum = jnp.dot(log_keep, upper, precision=precise, preferred_element_type=jnp.float32)
        return start, blk, live, delta_x, delta_y, falloff, alpha, log_keep, cum

    def chunk(c, carry):
        first = pl.multiple_of(c * PC, PC)
        q = first + lax.broadcasted_iota(jnp.int32, (PC, KB), 0)
        pix_x = (base_x + q % TILE_SIDE).astype(jnp.float32) + 0.5
        pix_y = (base_y + q // TILE_SIDE).astype(jnp.float32) + 0.5

        def forward(i, fc):
            log_total, color = fc
            start, blk, live, dx, dy, fall, alpha, lk, cum = terms(i, pix_x, pix_y)
            weight = jnp.exp(log_total + cum - lk) * alpha
            color = color + lax.dot_general(weight, blk[8:16], (((1,), (1,)), ((), ())), precision=precise, preferred_element_type=jnp.float32)
            return (log_total + cum[:, KB - 1:KB], color)

        log_total, color = lax.fori_loop(0, blocks, forward, (jnp.zeros((PC, 1), jnp.float32), jnp.zeros((PC, 8), jnp.float32)))
        image = color + jnp.exp(log_total) * bg
        image_ref[pl.ds(first, PC), :] = image
        resid = image - target_ref[pl.ds(first, PC), :]
        dot_total = jnp.sum(image * resid, axis=1, keepdims=True)

        def backward(i, bc):
            log_before, prefix = bc
            start, blk, live, dx, dy, fall, alpha, lk, cum = terms(i, pix_x, pix_y)
            trans = jnp.exp(log_before + cum - lk)
            weight = trans * alpha
            along = jnp.dot(resid, blk[8:16], precision=precise, preferred_element_type=jnp.float32)
            running = prefix + jnp.dot(weight * along, upper, precision=precise, preferred_element_type=jnp.float32)
            d_alpha = jnp.where(live, trans * along - (dot_total - running) / (1.0 - alpha), 0.0)
            d_power = d_alpha * alpha
            px_term = d_power * dx
            py_term = d_power * dy
            parts = [
                px_term, py_term, px_term * dx, px_term * dy, py_term * dy, d_alpha * fall,
                weight * resid[:, 0:1], weight * resid[:, 1:2], weight * resid[:, 2:3],
            ]
            for r, part in enumerate(parts):
                sums_ref[r:r + 1, pl.ds(start, KB)] += jnp.sum(part, axis=0, keepdims=True)
            return (log_before + cum[:, KB - 1:KB], running[:, KB - 1:KB])

        lax.fori_loop(0, blocks, backward, (jnp.zeros((PC, 1), jnp.float32), jnp.zeros((PC, 1), jnp.float32)))
        return carry

    lax.fori_loop(0, PIXELS // PC, chunk, 0)


def render_tiles(entry16, counts, tiles, target8, bg8, tile_cols):
    n = entry16.shape[0]
    return pl.pallas_call(
        partial(render_kernel, tile_cols=tile_cols),
        grid=(n,),
        in_specs=[
            pl.BlockSpec(memory_space=pltpu.SMEM),
            pl.BlockSpec(memory_space=pltpu.SMEM),
            pl.BlockSpec((None, 16, LIST), lambda t: (t, 0, 0)),
            pl.BlockSpec((None, PIXELS, 8), lambda t: (t, 0, 0)),
            pl.BlockSpec((1, 8), lambda t: (0, 0)),
        ],
        out_specs=[
            pl.BlockSpec((None, PIXELS, 8), lambda t: (t, 0, 0)),
            pl.BlockSpec((None, 16, LIST), lambda t: (t, 0, 0)),
        ],
        out_shape=[
            jax.ShapeDtypeStruct((n, PIXELS, 8), jnp.float32),
            jax.ShapeDtypeStruct((n, 16, LIST), jnp.float32),
        ],
    )(counts, tiles, entry16, target8, bg8)


def adam_step(values, first, second, grad, rates):
    first_new = decay_one * first + (1.0 - decay_one) * grad
    second_new = decay_two * second + (1.0 - decay_two) * grad * grad
    return (
        values - rates[:, None] * first_new / (jnp.sqrt(second_new) + adam_epsilon),
        first_new,
        second_new,
    )


def body(
    gaussians,
    moment_one,
    moment_two,
    learn_rates,
    cameras,
    camera_ids,
    list_owner,
    list_index,
    list_length,
    targets,
    background,
):
    peers = lax.axis_size("tiles")
    tiles_here = list_index.shape[1]
    entries = tiles_here * LIST
    owned = gaussians.shape[1]
    capacity = 2 * entries // peers
    tile_cols = tiles_here * peers // TILE_ROWS
    center_x = 0.5 * TILE_SIDE * tile_cols
    center_y = 0.5 * TILE_SIDE * TILE_ROWS
    camera = cameras[camera_ids[0]]
    attrs = project(gaussians, camera, center_x, center_y)
    owner_flat = list_owner.reshape(-1)
    index_flat = list_index.reshape(-1)
    earlier = jnp.arange(entries)[None, :] < jnp.arange(entries)[:, None]
    same = owner_flat[:, None] == owner_flat[None, :]
    rank = jnp.sum((same & earlier).astype(jnp.int32), axis=1)
    slot = owner_flat * capacity + rank
    asked_for = (
        jnp.zeros((peers * capacity,), jnp.int32)
        .at[slot]
        .set(index_flat, unique_indices=True)
        .reshape(peers, capacity)
    )
    asked = lax.all_to_all(asked_for, "tiles", split_axis=0, concat_axis=0, tiled=True)
    served = jnp.take(attrs, asked, axis=1)
    returned = lax.all_to_all(served, "tiles", split_axis=1, concat_axis=1, tiled=True)
    entry_attrs = returned.reshape(9, peers * capacity)[:, slot].reshape(9, tiles_here, LIST)
    first_tile = lax.axis_index("tiles") * tiles_here

    colors_pad = jnp.zeros((5, tiles_here, LIST), jnp.float32)
    entry16 = jnp.moveaxis(
        jnp.concatenate([entry_attrs[0:6], colors_pad[0:2], entry_attrs[6:9], colors_pad], axis=0), 1, 0
    )
    target8 = jnp.pad(
        jnp.swapaxes(targets[0].astype(jnp.float32), 1, 2), ((0, 0), (0, 0), (0, 5))
    )
    background8 = jnp.pad(background, (0, 5))[None]
    tile_ids = first_tile + jnp.arange(tiles_here, dtype=jnp.int32)
    image8, sums = render_tiles(entry16, list_length[0], tile_ids, target8, background8, tile_cols)
    images = jnp.swapaxes(image8[:, :, 0:3], 1, 2)
    sums = jnp.moveaxis(sums, 1, 0).reshape(16, entries)
    flat = entry_attrs.reshape(9, entries)
    flat_grads = jnp.stack(
        [
            flat[2] * sums[0] + flat[3] * sums[1],
            flat[3] * sums[0] + flat[4] * sums[1],
            -0.5 * sums[2],
            -sums[3],
            -0.5 * sums[4],
            sums[5],
            sums[6],
            sums[7],
            sums[8],
        ]
    )
    grad_send = (
        jnp.zeros((9, peers * capacity), jnp.float32)
        .at[:, slot]
        .set(flat_grads, unique_indices=True)
        .reshape(9, peers, capacity)
    )
    grad_back = lax.all_to_all(grad_send, "tiles", split_axis=1, concat_axis=1, tiled=True)
    attr_grad = (
        jnp.zeros((9, owned), jnp.float32)
        .at[:, asked.reshape(-1)]
        .add(grad_back.reshape(9, peers * capacity))
    )
    payload = jnp.concatenate([attr_grad.reshape(-1), jnp.pad(camera, (0, 128 - 12))])
    gathered = lax.all_gather(payload.reshape(-1, 128), "views", axis=0, tiled=False)
    gathered = gathered.reshape(gathered.shape[0], -1)
    view_grads = gathered[:, : 9 * owned].reshape(-1, 9, owned)
    view_cameras = gathered[:, 9 * owned : 9 * owned + 12]

    def pull(view_camera, grad):
        ignored, pullback = jax.vjp(
            partial(project, camera=view_camera, center_x=center_x, center_y=center_y),
            gaussians,
        )
        return pullback(grad)[0]

    total = jnp.sum(jax.vmap(pull)(view_cameras, view_grads), axis=0)
    new_values, first_new, second_new = adam_step(
        gaussians, moment_one, moment_two, total, learn_rates
    )
    return (images[None].astype(jnp.bfloat16), new_values, first_new, second_new)


def solution(mesh):
    return jax.shard_map(
        body,
        mesh=mesh,
        in_specs=(
            P(None, "tiles"),
            P(None, "tiles"),
            P(None, "tiles"),
            P(),
            P(),
            P("views"),
            P("views", "tiles", None, None),
            P("views", "tiles", None),
            P("views", "tiles"),
            P("views", "tiles", None, None),
            P(),
        ),
        out_specs=(
            P("views", "tiles", None, None),
            P(None, "tiles"),
            P(None, "tiles"),
            P(None, "tiles"),
        ),
        check_vma=False,
    )
```

```python
from functools import partial

import jax
import jax.numpy as jnp
from jax import lax
from jax.experimental import pallas as pl
from jax.experimental.pallas import tpu as pltpu
from jax.sharding import PartitionSpec as P

TILE_SIDE = 32
PIXELS = 1024
TILE_ROWS = 8
LIST = 1024
BLOCK = 128
KB = 128


focal_length = 400.0
precise = lax.Precision.HIGHEST
decay_one = 0.9
decay_two = 0.999
adam_epsilon = 1e-08


def sh_basis(direction):
    dir_x, dir_y, dir_z = (direction[0], direction[1], direction[2])
    sq_x, sq_y, sq_z = (dir_x * dir_x, dir_y * dir_y, dir_z * dir_z)
    terms = [
        0.28209479177387814 * jnp.ones_like(dir_x),
        -0.4886025119029199 * dir_y,
        0.4886025119029199 * dir_z,
        -0.4886025119029199 * dir_x,
        1.0925484305920792 * dir_x * dir_y,
        -1.0925484305920792 * dir_y * dir_z,
        0.31539156525252005 * (2.0 * sq_z - sq_x - sq_y),
        -1.0925484305920792 * dir_x * dir_z,
        0.5462742152960396 * (sq_x - sq_y),
        -0.5900435899266435 * dir_y * (3.0 * sq_x - sq_y),
        2.890611442640554 * dir_x * dir_y * dir_z,
        -0.4570457994644658 * dir_y * (4.0 * sq_z - sq_x - sq_y),
        0.3731763325901154 * dir_z * (2.0 * sq_z - 3.0 * sq_x - 3.0 * sq_y),
        -0.4570457994644658 * dir_x * (4.0 * sq_z - sq_x - sq_y),
        1.445305721320277 * dir_z * (sq_x - sq_y),
        -0.5900435899266435 * dir_x * (sq_x - 3.0 * sq_y),
    ]
    return jnp.stack(terms)


def quat_rotation(quat):
    length = jnp.sqrt(jnp.sum(quat * quat, axis=0))
    quat_w, quat_x, quat_y, quat_z = (
        quat[0] / length,
        quat[1] / length,
        quat[2] / length,
        quat[3] / length,
    )
    rows = [
        [
            1.0 - 2.0 * (quat_y * quat_y + quat_z * quat_z),
            2.0 * (quat_x * quat_y - quat_w * quat_z),
            2.0 * (quat_x * quat_z + quat_w * quat_y),
        ],
        [
            2.0 * (quat_x * quat_y + quat_w * quat_z),
            1.0 - 2.0 * (quat_x * quat_x + quat_z * quat_z),
            2.0 * (quat_y * quat_z - quat_w * quat_x),
        ],
        [
            2.0 * (quat_x * quat_z - quat_w * quat_y),
            2.0 * (quat_y * quat_z + quat_w * quat_x),
            1.0 - 2.0 * (quat_x * quat_x + quat_y * quat_y),
        ],
    ]
    return jnp.stack([jnp.stack(entries) for entries in rows])


def project(params, camera, center_x, center_y):
    means = params[0:3]
    rotate = camera[0:9].reshape(3, 3)
    shift = camera[9:12]
    view_pos = jnp.dot(rotate, means, precision=precise) + shift[:, None]
    inv_depth = 1.0 / view_pos[2]
    image_x = focal_length * view_pos[0] * inv_depth + center_x
    image_y = focal_length * view_pos[1] * inv_depth + center_y
    scales = jnp.exp(params[3:6])
    local_axes = quat_rotation(params[6:10]) * scales[None, :, :]
    world_axes = jnp.einsum("ik,kjg->ijg", rotate, local_axes, precision=precise)
    proj_x = (
        focal_length * inv_depth * world_axes[0]
        - focal_length * view_pos[0] * inv_depth * inv_depth * world_axes[2]
    )
    proj_y = (
        focal_length * inv_depth * world_axes[1]
        - focal_length * view_pos[1] * inv_depth * inv_depth * world_axes[2]
    )
    cov_xx = jnp.sum(proj_x * proj_x, axis=0) + 0.3
    cov_xy = jnp.sum(proj_x * proj_y, axis=0)
    cov_yy = jnp.sum(proj_y * proj_y, axis=0) + 0.3
    determ = cov_xx * cov_yy - cov_xy * cov_xy
    opacity = 0.99 * jax.nn.sigmoid(params[10])
    center = -jnp.dot(rotate.T, shift, precision=precise)
    offset = means - center[:, None]
    direction = offset / jnp.sqrt(jnp.sum(offset * offset, axis=0))
    basis = sh_basis(direction)
    coeffs = params[11:59].reshape(16, 3, -1)
    colors = 0.5 + jnp.sum(basis[:, None, :] * coeffs, axis=0)
    head = jnp.stack(
        [image_x, image_y, cov_yy / determ, -cov_xy / determ, cov_xx / determ, opacity]
    )
    return jnp.concatenate([head, colors], axis=0)


def pixel_grid(tile, tile_cols):
    offsets = jnp.arange(PIXELS)
    pixel_x = (tile % tile_cols * TILE_SIDE + offsets % TILE_SIDE).astype(jnp.float32) + 0.5
    pixel_y = (tile // tile_cols * TILE_SIDE + offsets // TILE_SIDE).astype(jnp.float32) + 0.5
    return (pixel_x, pixel_y)


def block_terms(entry, count, pixel_x, pixel_y, index):
    start = index * BLOCK
    piece = lax.dynamic_slice_in_dim(entry, start, BLOCK, 1)
    live = (start + jnp.arange(BLOCK) < count)[None, :]
    delta_x = pixel_x[:, None] - piece[0][None, :]
    delta_y = pixel_y[:, None] - piece[1][None, :]
    power = -0.5 * (
        piece[2] * delta_x * delta_x
        + 2.0 * piece[3] * delta_x * delta_y
        + piece[4] * delta_y * delta_y
    )
    falloff = jnp.exp(power)
    alpha = jnp.where(live, piece[5][None, :] * falloff, 0.0)
    log_keep = jnp.log1p(-alpha)
    return (start, piece, live, delta_x, delta_y, falloff, alpha, log_keep)


def tile_pass(entry, count, pixel_x, pixel_y, target, background):
    blocks = (count + BLOCK - 1) // BLOCK

    def forward(index, carry):
        color, log_total = carry
        start, piece, live, delta_x, delta_y, falloff, alpha, log_keep = block_terms(
            entry, count, pixel_x, pixel_y, index
        )
        weight = jnp.exp(log_total[:, None] + jnp.cumsum(log_keep, axis=1) - log_keep) * alpha
        color = color + lax.dot_general(
            piece[6:9], weight, (((1,), (1,)), ((), ())), precision=precise
        )
        return (color, log_total + jnp.sum(log_keep, axis=1))

    zeros_pix = jnp.zeros((PIXELS,), jnp.float32)
    color, log_total = lax.fori_loop(
        0, blocks, forward, (jnp.zeros((3, PIXELS), jnp.float32), zeros_pix)
    )
    image = color + jnp.exp(log_total)[None, :] * background[:, None]
    resid = image - target
    dot_total = jnp.sum(image * resid, axis=0)

    def backward(index, carry):
        grads, log_before, prefix = carry
        start, piece, live, delta_x, delta_y, falloff, alpha, log_keep = block_terms(
            entry, count, pixel_x, pixel_y, index
        )
        trans = jnp.exp(log_before[:, None] + jnp.cumsum(log_keep, axis=1) - log_keep)
        weight = trans * alpha
        along = lax.dot_general(resid, piece[6:9], (((0,), (0,)), ((), ())), precision=precise)
        running = prefix[:, None] + jnp.cumsum(weight * along, axis=1)
        d_alpha = jnp.where(
            live, trans * along - (dot_total[:, None] - running) / (1.0 - alpha), 0.0
        )
        d_power = d_alpha * alpha
        sum_x = jnp.sum(d_power * delta_x, axis=0)
        sum_y = jnp.sum(d_power * delta_y, axis=0)
        head = jnp.stack(
            [
                piece[2] * sum_x + piece[3] * sum_y,
                piece[3] * sum_x + piece[4] * sum_y,
                -0.5 * jnp.sum(d_power * delta_x * delta_x, axis=0),
                -jnp.sum(d_power * delta_x * delta_y, axis=0),
                -0.5 * jnp.sum(d_power * delta_y * delta_y, axis=0),
                jnp.sum(d_alpha * falloff, axis=0),
            ]
        )
        color_grad = jnp.dot(resid, weight, precision=precise)
        block_grad = jnp.concatenate([head, color_grad], axis=0)
        grads = lax.dynamic_update_slice_in_dim(grads, block_grad, start, 1)
        return (grads, log_before + jnp.sum(log_keep, axis=1), running[:, -1])

    start_grads = jnp.zeros((9, LIST), jnp.float32)
    grads, ignored, unused = lax.fori_loop(0, blocks, backward, (start_grads, zeros_pix, zeros_pix))
    return (image, grads)


def split_cumsum(x, upper):
    high = x.astype(jnp.bfloat16)
    rest = x - high.astype(jnp.float32)
    middle = rest.astype(jnp.bfloat16)
    low = (rest - middle.astype(jnp.float32)).astype(jnp.bfloat16)
    total = jnp.dot(high, upper, preferred_element_type=jnp.float32)
    total = total + jnp.dot(middle, upper, preferred_element_type=jnp.float32)
    return total + jnp.dot(low, upper, preferred_element_type=jnp.float32)


def render_kernel(
    counts_ref, tiles_ref, entry_ref, target_ref, bg_ref, image_ref, sums_ref, trans_ref, fall_ref, *, tile_cols
):
    t = pl.program_id(0)
    count = counts_ref[t]
    tile = tiles_ref[t]
    blocks = (count + KB - 1) // KB
    sums_ref[...] = jnp.zeros(sums_ref.shape, jnp.float32)
    row = lax.broadcasted_iota(jnp.int32, (KB, KB), 0)
    col = lax.broadcasted_iota(jnp.int32, (KB, KB), 1)
    upper = (row <= col).astype(jnp.bfloat16)
    lane = lax.broadcasted_iota(jnp.int32, (1, KB), 1)
    pixel = lax.broadcasted_iota(jnp.int32, (PIXELS, KB), 0)
    pix_x = ((tile % tile_cols) * TILE_SIDE + pixel % TILE_SIDE).astype(jnp.float32) + 0.5
    pix_y = ((tile // tile_cols) * TILE_SIDE + pixel // TILE_SIDE).astype(jnp.float32) + 0.5

    def geometry(index):
        start = pl.multiple_of(index * KB, KB)
        blk = entry_ref[:, pl.ds(start, KB)]
        live = (start + lane) < count
        return start, blk, live, pix_x - blk[0:1], pix_y - blk[1:2]

    def forward(i, carry):
        log_total, red, green, blue = carry
        start, blk, live, dx, dy = geometry(i)
        power = -0.5 * (blk[2:3] * dx * dx + 2.0 * blk[3:4] * dx * dy + blk[4:5] * dy * dy)
        falloff = jnp.exp(power)
        alpha = jnp.where(live, blk[5:6] * falloff, 0.0)
        log_keep = jnp.log1p(-alpha)
        cum = split_cumsum(log_keep, upper)
        trans = jnp.exp(log_total + cum - log_keep)
        weight = trans * alpha
        trans_ref[:, pl.ds(start, KB)] = trans
        fall_ref[:, pl.ds(start, KB)] = falloff
        return (
            log_total + cum[:, KB - 1 : KB],
            red + weight * blk[8:9],
            green + weight * blk[9:10],
            blue + weight * blk[10:11],
        )

    zeros = jnp.zeros((PIXELS, KB), jnp.float32)
    log_total, red, green, blue = lax.fori_loop(
        0, blocks, forward, (jnp.zeros((PIXELS, 1), jnp.float32), zeros, zeros, zeros)
    )
    lane8 = lax.broadcasted_iota(jnp.int32, (1, 8), 1)
    color = (
        jnp.where(lane8 == 0, jnp.sum(red, axis=1, keepdims=True), 0.0)
        + jnp.where(lane8 == 1, jnp.sum(green, axis=1, keepdims=True), 0.0)
        + jnp.where(lane8 == 2, jnp.sum(blue, axis=1, keepdims=True), 0.0)
    )
    image = color + jnp.exp(log_total) * bg_ref[...]
    image_ref[...] = image
    resid = image - target_ref[...]
    dot_total = jnp.sum(image * resid, axis=1, keepdims=True)
    resid_r, resid_g, resid_b = resid[:, 0:1], resid[:, 1:2], resid[:, 2:3]

    def backward(i, prefix):
        start, blk, live, dx, dy = geometry(i)
        trans = trans_ref[:, pl.ds(start, KB)]
        falloff = fall_ref[:, pl.ds(start, KB)]
        alpha = jnp.where(live, blk[5:6] * falloff, 0.0)
        weight = trans * alpha
        along = resid_r * blk[8:9] + resid_g * blk[9:10] + resid_b * blk[10:11]
        running = prefix + split_cumsum(weight * along, upper)
        d_alpha = jnp.where(live, trans * along - (dot_total - running) / (1.0 - alpha), 0.0)
        d_power = d_alpha * alpha
        x_term = d_power * dx
        y_term = d_power * dy
        parts = [
            x_term,
            y_term,
            x_term * dx,
            x_term * dy,
            y_term * dy,
            d_alpha * falloff,
            weight * resid_r,
            weight * resid_g,
            weight * resid_b,
        ]
        for r, part in enumerate(parts):
            sums_ref[r : r + 1, pl.ds(start, KB)] += jnp.sum(part, axis=0, keepdims=True)
        return running[:, KB - 1 : KB]

    lax.fori_loop(0, blocks, backward, jnp.zeros((PIXELS, 1), jnp.float32))


def render_tiles(entry16, counts, tiles, target8, bg8, tile_cols):
    n = entry16.shape[0]
    return pl.pallas_call(
        partial(render_kernel, tile_cols=tile_cols),
        grid=(n,),
        in_specs=[
            pl.BlockSpec(memory_space=pltpu.SMEM),
            pl.BlockSpec(memory_space=pltpu.SMEM),
            pl.BlockSpec((None, 16, LIST), lambda t: (t, 0, 0)),
            pl.BlockSpec((None, PIXELS, 8), lambda t: (t, 0, 0)),
            pl.BlockSpec((1, 8), lambda t: (0, 0)),
        ],
        out_specs=[
            pl.BlockSpec((None, PIXELS, 8), lambda t: (t, 0, 0)),
            pl.BlockSpec((None, 16, LIST), lambda t: (t, 0, 0)),
        ],
        out_shape=[
            jax.ShapeDtypeStruct((n, PIXELS, 8), jnp.float32),
            jax.ShapeDtypeStruct((n, 16, LIST), jnp.float32),
        ],
        scratch_shapes=[
            pltpu.VMEM((PIXELS, LIST), jnp.float32),
            pltpu.VMEM((PIXELS, LIST), jnp.float32),
        ],
    )(counts, tiles, entry16, target8, bg8)


def adam_step(values, first, second, grad, rates):
    first_new = decay_one * first + (1.0 - decay_one) * grad
    second_new = decay_two * second + (1.0 - decay_two) * grad * grad
    return (
        values - rates[:, None] * first_new / (jnp.sqrt(second_new) + adam_epsilon),
        first_new,
        second_new,
    )


def body(
    gaussians,
    moment_one,
    moment_two,
    learn_rates,
    cameras,
    camera_ids,
    list_owner,
    list_index,
    list_length,
    targets,
    background,
):
    peers = lax.axis_size("tiles")
    tiles_here = list_index.shape[1]
    entries = tiles_here * LIST
    owned = gaussians.shape[1]
    capacity = 2 * entries // peers
    tile_cols = tiles_here * peers // TILE_ROWS
    center_x = 0.5 * TILE_SIDE * tile_cols
    center_y = 0.5 * TILE_SIDE * TILE_ROWS
    camera = cameras[camera_ids[0]]
    attrs = project(gaussians, camera, center_x, center_y)
    owner_flat = list_owner.reshape(-1)
    index_flat = list_index.reshape(-1)
    earlier = jnp.arange(entries)[None, :] < jnp.arange(entries)[:, None]
    same = owner_flat[:, None] == owner_flat[None, :]
    rank = jnp.sum((same & earlier).astype(jnp.int32), axis=1)
    slot = owner_flat * capacity + rank
    asked_for = (
        jnp.zeros((peers * capacity,), jnp.int32)
        .at[slot]
        .set(index_flat, unique_indices=True)
        .reshape(peers, capacity)
    )
    asked = lax.all_to_all(asked_for, "tiles", split_axis=0, concat_axis=0, tiled=True)
    served = jnp.take(attrs, asked, axis=1)
    returned = lax.all_to_all(served, "tiles", split_axis=1, concat_axis=1, tiled=True)
    entry_attrs = returned.reshape(9, peers * capacity)[:, slot].reshape(9, tiles_here, LIST)
    first_tile = lax.axis_index("tiles") * tiles_here

    colors_pad = jnp.zeros((5, tiles_here, LIST), jnp.float32)
    entry16 = jnp.moveaxis(
        jnp.concatenate([entry_attrs[0:6], colors_pad[0:2], entry_attrs[6:9], colors_pad], axis=0), 1, 0
    )
    target8 = jnp.pad(
        jnp.swapaxes(targets[0].astype(jnp.float32), 1, 2), ((0, 0), (0, 0), (0, 5))
    )
    background8 = jnp.pad(background, (0, 5))[None]
    tile_ids = first_tile + jnp.arange(tiles_here, dtype=jnp.int32)
    image8, sums = render_tiles(entry16, list_length[0], tile_ids, target8, background8, tile_cols)
    images = jnp.swapaxes(image8[:, :, 0:3], 1, 2)
    sums = jnp.moveaxis(sums, 1, 0).reshape(16, entries)
    flat = entry_attrs.reshape(9, entries)
    flat_grads = jnp.stack(
        [
            flat[2] * sums[0] + flat[3] * sums[1],
            flat[3] * sums[0] + flat[4] * sums[1],
            -0.5 * sums[2],
            -sums[3],
            -0.5 * sums[4],
            sums[5],
            sums[6],
            sums[7],
            sums[8],
        ]
    )
    grad_send = (
        jnp.zeros((9, peers * capacity), jnp.float32)
        .at[:, slot]
        .set(flat_grads, unique_indices=True)
        .reshape(9, peers, capacity)
    )
    grad_back = lax.all_to_all(grad_send, "tiles", split_axis=1, concat_axis=1, tiled=True)
    attr_grad = (
        jnp.zeros((9, owned), jnp.float32)
        .at[:, asked.reshape(-1)]
        .add(grad_back.reshape(9, peers * capacity))
    )
    payload = jnp.concatenate([attr_grad.reshape(-1), jnp.pad(camera, (0, 128 - 12))])
    gathered = lax.all_gather(payload.reshape(-1, 128), "views", axis=0, tiled=False)
    gathered = gathered.reshape(gathered.shape[0], -1)
    view_grads = gathered[:, : 9 * owned].reshape(-1, 9, owned)
    view_cameras = gathered[:, 9 * owned : 9 * owned + 12]

    def pull(view_camera, grad):
        ignored, pullback = jax.vjp(
            partial(project, camera=view_camera, center_x=center_x, center_y=center_y),
            gaussians,
        )
        return pullback(grad)[0]

    total = jnp.sum(jax.vmap(pull)(view_cameras, view_grads), axis=0)
    new_values, first_new, second_new = adam_step(
        gaussians, moment_one, moment_two, total, learn_rates
    )
    return (images[None].astype(jnp.bfloat16), new_values, first_new, second_new)


def solution(mesh):
    return jax.shard_map(
        body,
        mesh=mesh,
        in_specs=(
            P(None, "tiles"),
            P(None, "tiles"),
            P(None, "tiles"),
            P(),
            P(),
            P("views"),
            P("views", "tiles", None, None),
            P("views", "tiles", None),
            P("views", "tiles"),
            P("views", "tiles", None, None),
            P(),
        ),
        out_specs=(
            P("views", "tiles", None, None),
            P(None, "tiles"),
            P(None, "tiles"),
            P(None, "tiles"),
        ),
        check_vma=False,
    )
```

```python
from functools import partial

import jax
import jax.numpy as jnp
from jax import lax
from jax.experimental import pallas as pl
from jax.experimental.pallas import tpu as pltpu
from jax.sharding import PartitionSpec as P

TILE_SIDE = 32
PIXELS = 1024
TILE_ROWS = 8
LIST = 1024
BLOCK = 128
KB = 128


focal_length = 400.0
precise = lax.Precision.HIGHEST
decay_one = 0.9
decay_two = 0.999
adam_epsilon = 1e-08


def sh_basis(direction):
    dir_x, dir_y, dir_z = (direction[0], direction[1], direction[2])
    sq_x, sq_y, sq_z = (dir_x * dir_x, dir_y * dir_y, dir_z * dir_z)
    terms = [
        0.28209479177387814 * jnp.ones_like(dir_x),
        -0.4886025119029199 * dir_y,
        0.4886025119029199 * dir_z,
        -0.4886025119029199 * dir_x,
        1.0925484305920792 * dir_x * dir_y,
        -1.0925484305920792 * dir_y * dir_z,
        0.31539156525252005 * (2.0 * sq_z - sq_x - sq_y),
        -1.0925484305920792 * dir_x * dir_z,
        0.5462742152960396 * (sq_x - sq_y),
        -0.5900435899266435 * dir_y * (3.0 * sq_x - sq_y),
        2.890611442640554 * dir_x * dir_y * dir_z,
        -0.4570457994644658 * dir_y * (4.0 * sq_z - sq_x - sq_y),
        0.3731763325901154 * dir_z * (2.0 * sq_z - 3.0 * sq_x - 3.0 * sq_y),
        -0.4570457994644658 * dir_x * (4.0 * sq_z - sq_x - sq_y),
        1.445305721320277 * dir_z * (sq_x - sq_y),
        -0.5900435899266435 * dir_x * (sq_x - 3.0 * sq_y),
    ]
    return jnp.stack(terms)


def quat_rotation(quat):
    length = jnp.sqrt(jnp.sum(quat * quat, axis=0))
    quat_w, quat_x, quat_y, quat_z = (
        quat[0] / length,
        quat[1] / length,
        quat[2] / length,
        quat[3] / length,
    )
    rows = [
        [
            1.0 - 2.0 * (quat_y * quat_y + quat_z * quat_z),
            2.0 * (quat_x * quat_y - quat_w * quat_z),
            2.0 * (quat_x * quat_z + quat_w * quat_y),
        ],
        [
            2.0 * (quat_x * quat_y + quat_w * quat_z),
            1.0 - 2.0 * (quat_x * quat_x + quat_z * quat_z),
            2.0 * (quat_y * quat_z - quat_w * quat_x),
        ],
        [
            2.0 * (quat_x * quat_z - quat_w * quat_y),
            2.0 * (quat_y * quat_z + quat_w * quat_x),
            1.0 - 2.0 * (quat_x * quat_x + quat_y * quat_y),
        ],
    ]
    return jnp.stack([jnp.stack(entries) for entries in rows])


def project(params, camera, center_x, center_y):
    means = params[0:3]
    rotate = camera[0:9].reshape(3, 3)
    shift = camera[9:12]
    view_pos = jnp.dot(rotate, means, precision=precise) + shift[:, None]
    inv_depth = 1.0 / view_pos[2]
    image_x = focal_length * view_pos[0] * inv_depth + center_x
    image_y = focal_length * view_pos[1] * inv_depth + center_y
    scales = jnp.exp(params[3:6])
    local_axes = quat_rotation(params[6:10]) * scales[None, :, :]
    world_axes = jnp.einsum("ik,kjg->ijg", rotate, local_axes, precision=precise)
    proj_x = (
        focal_length * inv_depth * world_axes[0]
        - focal_length * view_pos[0] * inv_depth * inv_depth * world_axes[2]
    )
    proj_y = (
        focal_length * inv_depth * world_axes[1]
        - focal_length * view_pos[1] * inv_depth * inv_depth * world_axes[2]
    )
    cov_xx = jnp.sum(proj_x * proj_x, axis=0) + 0.3
    cov_xy = jnp.sum(proj_x * proj_y, axis=0)
    cov_yy = jnp.sum(proj_y * proj_y, axis=0) + 0.3
    determ = cov_xx * cov_yy - cov_xy * cov_xy
    opacity = 0.99 * jax.nn.sigmoid(params[10])
    center = -jnp.dot(rotate.T, shift, precision=precise)
    offset = means - center[:, None]
    direction = offset / jnp.sqrt(jnp.sum(offset * offset, axis=0))
    basis = sh_basis(direction)
    coeffs = params[11:59].reshape(16, 3, -1)
    colors = 0.5 + jnp.sum(basis[:, None, :] * coeffs, axis=0)
    head = jnp.stack(
        [image_x, image_y, cov_yy / determ, -cov_xy / determ, cov_xx / determ, opacity]
    )
    return jnp.concatenate([head, colors], axis=0)


def pixel_grid(tile, tile_cols):
    offsets = jnp.arange(PIXELS)
    pixel_x = (tile % tile_cols * TILE_SIDE + offsets % TILE_SIDE).astype(jnp.float32) + 0.5
    pixel_y = (tile // tile_cols * TILE_SIDE + offsets // TILE_SIDE).astype(jnp.float32) + 0.5
    return (pixel_x, pixel_y)


def block_terms(entry, count, pixel_x, pixel_y, index):
    start = index * BLOCK
    piece = lax.dynamic_slice_in_dim(entry, start, BLOCK, 1)
    live = (start + jnp.arange(BLOCK) < count)[None, :]
    delta_x = pixel_x[:, None] - piece[0][None, :]
    delta_y = pixel_y[:, None] - piece[1][None, :]
    power = -0.5 * (
        piece[2] * delta_x * delta_x
        + 2.0 * piece[3] * delta_x * delta_y
        + piece[4] * delta_y * delta_y
    )
    falloff = jnp.exp(power)
    alpha = jnp.where(live, piece[5][None, :] * falloff, 0.0)
    log_keep = jnp.log1p(-alpha)
    return (start, piece, live, delta_x, delta_y, falloff, alpha, log_keep)


def tile_pass(entry, count, pixel_x, pixel_y, target, background):
    blocks = (count + BLOCK - 1) // BLOCK

    def forward(index, carry):
        color, log_total = carry
        start, piece, live, delta_x, delta_y, falloff, alpha, log_keep = block_terms(
            entry, count, pixel_x, pixel_y, index
        )
        weight = jnp.exp(log_total[:, None] + jnp.cumsum(log_keep, axis=1) - log_keep) * alpha
        color = color + lax.dot_general(
            piece[6:9], weight, (((1,), (1,)), ((), ())), precision=precise
        )
        return (color, log_total + jnp.sum(log_keep, axis=1))

    zeros_pix = jnp.zeros((PIXELS,), jnp.float32)
    color, log_total = lax.fori_loop(
        0, blocks, forward, (jnp.zeros((3, PIXELS), jnp.float32), zeros_pix)
    )
    image = color + jnp.exp(log_total)[None, :] * background[:, None]
    resid = image - target
    dot_total = jnp.sum(image * resid, axis=0)

    def backward(index, carry):
        grads, log_before, prefix = carry
        start, piece, live, delta_x, delta_y, falloff, alpha, log_keep = block_terms(
            entry, count, pixel_x, pixel_y, index
        )
        trans = jnp.exp(log_before[:, None] + jnp.cumsum(log_keep, axis=1) - log_keep)
        weight = trans * alpha
        along = lax.dot_general(resid, piece[6:9], (((0,), (0,)), ((), ())), precision=precise)
        running = prefix[:, None] + jnp.cumsum(weight * along, axis=1)
        d_alpha = jnp.where(
            live, trans * along - (dot_total[:, None] - running) / (1.0 - alpha), 0.0
        )
        d_power = d_alpha * alpha
        sum_x = jnp.sum(d_power * delta_x, axis=0)
        sum_y = jnp.sum(d_power * delta_y, axis=0)
        head = jnp.stack(
            [
                piece[2] * sum_x + piece[3] * sum_y,
                piece[3] * sum_x + piece[4] * sum_y,
                -0.5 * jnp.sum(d_power * delta_x * delta_x, axis=0),
                -jnp.sum(d_power * delta_x * delta_y, axis=0),
                -0.5 * jnp.sum(d_power * delta_y * delta_y, axis=0),
                jnp.sum(d_alpha * falloff, axis=0),
            ]
        )
        color_grad = jnp.dot(resid, weight, precision=precise)
        block_grad = jnp.concatenate([head, color_grad], axis=0)
        grads = lax.dynamic_update_slice_in_dim(grads, block_grad, start, 1)
        return (grads, log_before + jnp.sum(log_keep, axis=1), running[:, -1])

    start_grads = jnp.zeros((9, LIST), jnp.float32)
    grads, ignored, unused = lax.fori_loop(0, blocks, backward, (start_grads, zeros_pix, zeros_pix))
    return (image, grads)


def split_cumsum(x, upper):
    high = x.astype(jnp.bfloat16)
    rest = x - high.astype(jnp.float32)
    middle = rest.astype(jnp.bfloat16)
    low = (rest - middle.astype(jnp.float32)).astype(jnp.bfloat16)
    total = jnp.dot(high, upper, preferred_element_type=jnp.float32)
    total = total + jnp.dot(middle, upper, preferred_element_type=jnp.float32)
    return total + jnp.dot(low, upper, preferred_element_type=jnp.float32)


def render_kernel(
    counts_ref, tiles_ref, entry_ref, target_ref, bg_ref, image_ref, sums_ref, trans_ref, fall_ref, *, tile_cols
):
    t = pl.program_id(0)
    count = counts_ref[t]
    tile = tiles_ref[t]
    blocks = (count + KB - 1) // KB
    sums_ref[...] = jnp.zeros(sums_ref.shape, jnp.float32)
    row = lax.broadcasted_iota(jnp.int32, (KB, KB), 0)
    col = lax.broadcasted_iota(jnp.int32, (KB, KB), 1)
    upper = (row <= col).astype(jnp.bfloat16)
    lane = lax.broadcasted_iota(jnp.int32, (1, KB), 1)
    pixel = lax.broadcasted_iota(jnp.int32, (PIXELS, KB), 0)
    pix_x = ((tile % tile_cols) * TILE_SIDE + pixel % TILE_SIDE).astype(jnp.float32) + 0.5
    pix_y = ((tile // tile_cols) * TILE_SIDE + pixel // TILE_SIDE).astype(jnp.float32) + 0.5

    def geometry(index):
        start = pl.multiple_of(index * KB, KB)
        blk = entry_ref[:, pl.ds(start, KB)]
        live = (start + lane) < count
        return start, blk, live, pix_x - blk[0:1], pix_y - blk[1:2]

    def forward(i, carry):
        log_total, red, green, blue = carry
        start, blk, live, dx, dy = geometry(i)
        power = -0.5 * (blk[2:3] * dx * dx + 2.0 * blk[3:4] * dx * dy + blk[4:5] * dy * dy)
        falloff = jnp.exp(power)
        alpha = jnp.where(live, blk[5:6] * falloff, 0.0)
        log_keep = jnp.log1p(-alpha)
        cum = split_cumsum(log_keep, upper)
        trans = jnp.exp(log_total + cum - log_keep)
        weight = trans * alpha
        trans_ref[:, pl.ds(start, KB)] = trans
        fall_ref[:, pl.ds(start, KB)] = falloff
        return (
            log_total + cum[:, KB - 1 : KB],
            red + weight * blk[8:9],
            green + weight * blk[9:10],
            blue + weight * blk[10:11],
        )

    zeros = jnp.zeros((PIXELS, KB), jnp.float32)
    log_total, red, green, blue = lax.fori_loop(
        0, blocks, forward, (jnp.zeros((PIXELS, 1), jnp.float32), zeros, zeros, zeros)
    )
    lane8 = lax.broadcasted_iota(jnp.int32, (1, 8), 1)
    color = (
        jnp.where(lane8 == 0, jnp.sum(red, axis=1, keepdims=True), 0.0)
        + jnp.where(lane8 == 1, jnp.sum(green, axis=1, keepdims=True), 0.0)
        + jnp.where(lane8 == 2, jnp.sum(blue, axis=1, keepdims=True), 0.0)
    )
    image = color + jnp.exp(log_total) * bg_ref[...]
    image_ref[...] = image
    resid = image - target_ref[...]
    dot_total = jnp.sum(image * resid, axis=1, keepdims=True)
    resid_r, resid_g, resid_b = resid[:, 0:1], resid[:, 1:2], resid[:, 2:3]

    def backward(i, prefix):
        start, blk, live, dx, dy = geometry(i)
        trans = trans_ref[:, pl.ds(start, KB)]
        falloff = fall_ref[:, pl.ds(start, KB)]
        alpha = jnp.where(live, blk[5:6] * falloff, 0.0)
        weight = trans * alpha
        along = resid_r * blk[8:9] + resid_g * blk[9:10] + resid_b * blk[10:11]
        running = prefix + split_cumsum(weight * along, upper)
        d_alpha = jnp.where(live, trans * along - (dot_total - running) / (1.0 - alpha), 0.0)
        d_power = d_alpha * alpha
        x_term = d_power * dx
        y_term = d_power * dy
        parts = [
            x_term,
            y_term,
            x_term * dx,
            x_term * dy,
            y_term * dy,
            d_alpha * falloff,
            weight * resid_r,
            weight * resid_g,
            weight * resid_b,
        ]
        for r, part in enumerate(parts):
            sums_ref[r : r + 1, pl.ds(start, KB)] += jnp.sum(part, axis=0, keepdims=True)
        return running[:, KB - 1 : KB]

    lax.fori_loop(0, blocks, backward, jnp.zeros((PIXELS, 1), jnp.float32))


def render_tiles(entry16, counts, tiles, target8, bg8, tile_cols):
    n = entry16.shape[0]
    return pl.pallas_call(
        partial(render_kernel, tile_cols=tile_cols),
        grid=(n,),
        in_specs=[
            pl.BlockSpec(memory_space=pltpu.SMEM),
            pl.BlockSpec(memory_space=pltpu.SMEM),
            pl.BlockSpec((None, 16, LIST), lambda t: (t, 0, 0)),
            pl.BlockSpec((None, PIXELS, 8), lambda t: (t, 0, 0)),
            pl.BlockSpec((1, 8), lambda t: (0, 0)),
        ],
        out_specs=[
            pl.BlockSpec((None, PIXELS, 8), lambda t: (t, 0, 0)),
            pl.BlockSpec((None, 16, LIST), lambda t: (t, 0, 0)),
        ],
        out_shape=[
            jax.ShapeDtypeStruct((n, PIXELS, 8), jnp.float32),
            jax.ShapeDtypeStruct((n, 16, LIST), jnp.float32),
        ],
        scratch_shapes=[
            pltpu.VMEM((PIXELS, LIST), jnp.float32),
            pltpu.VMEM((PIXELS, LIST), jnp.float32),
        ],
    )(counts, tiles, entry16, target8, bg8)


def adam_step(values, first, second, grad, rates):
    first_new = decay_one * first + (1.0 - decay_one) * grad
    second_new = decay_two * second + (1.0 - decay_two) * grad * grad
    return (
        values - rates[:, None] * first_new / (jnp.sqrt(second_new) + adam_epsilon),
        first_new,
        second_new,
    )


def body(
    gaussians,
    moment_one,
    moment_two,
    learn_rates,
    cameras,
    camera_ids,
    list_owner,
    list_index,
    list_length,
    targets,
    background,
):
    peers = lax.axis_size("tiles")
    tiles_here = list_index.shape[1]
    entries = tiles_here * LIST
    owned = gaussians.shape[1]
    capacity = 2 * entries // peers
    tile_cols = tiles_here * peers // TILE_ROWS
    center_x = 0.5 * TILE_SIDE * tile_cols
    center_y = 0.5 * TILE_SIDE * TILE_ROWS
    camera = cameras[camera_ids[0]]
    attrs = project(gaussians, camera, center_x, center_y)
    owner_flat = list_owner.reshape(-1)
    index_flat = list_index.reshape(-1)
    earlier = jnp.arange(entries)[None, :] < jnp.arange(entries)[:, None]
    same = owner_flat[:, None] == owner_flat[None, :]
    rank = jnp.sum((same & earlier).astype(jnp.int32), axis=1)
    slot = owner_flat * capacity + rank
    asked_for = (
        jnp.zeros((peers * capacity,), jnp.int32)
        .at[slot]
        .set(index_flat, unique_indices=True)
        .reshape(peers, capacity)
    )
    asked = lax.all_to_all(asked_for, "tiles", split_axis=0, concat_axis=0, tiled=True)
    chosen = (asked.reshape(-1)[:, None] == jnp.arange(owned)[None, :]).astype(jnp.float32)
    served = lax.dot_general(
        attrs, chosen, (((1,), (1,)), ((), ())), precision=precise
    ).reshape(9, peers, capacity)
    returned = lax.all_to_all(served, "tiles", split_axis=1, concat_axis=1, tiled=True)
    entry_attrs = returned.reshape(9, peers * capacity)[:, slot].reshape(9, tiles_here, LIST)
    first_tile = lax.axis_index("tiles") * tiles_here

    colors_pad = jnp.zeros((5, tiles_here, LIST), jnp.float32)
    entry16 = jnp.moveaxis(
        jnp.concatenate([entry_attrs[0:6], colors_pad[0:2], entry_attrs[6:9], colors_pad], axis=0), 1, 0
    )
    target8 = jnp.pad(
        jnp.swapaxes(targets[0].astype(jnp.float32), 1, 2), ((0, 0), (0, 0), (0, 5))
    )
    background8 = jnp.pad(background, (0, 5))[None]
    tile_ids = first_tile + jnp.arange(tiles_here, dtype=jnp.int32)
    image8, sums = render_tiles(entry16, list_length[0], tile_ids, target8, background8, tile_cols)
    images = jnp.swapaxes(image8[:, :, 0:3], 1, 2)
    sums = jnp.moveaxis(sums, 1, 0).reshape(16, entries)
    flat = entry_attrs.reshape(9, entries)
    flat_grads = jnp.stack(
        [
            flat[2] * sums[0] + flat[3] * sums[1],
            flat[3] * sums[0] + flat[4] * sums[1],
            -0.5 * sums[2],
            -sums[3],
            -0.5 * sums[4],
            sums[5],
            sums[6],
            sums[7],
            sums[8],
        ]
    )
    grad_send = (
        jnp.zeros((9, peers * capacity), jnp.float32)
        .at[:, slot]
        .set(flat_grads, unique_indices=True)
        .reshape(9, peers, capacity)
    )
    grad_back = lax.all_to_all(grad_send, "tiles", split_axis=1, concat_axis=1, tiled=True)
    attr_grad = jnp.dot(grad_back.reshape(9, peers * capacity), chosen, precision=precise)
    payload = jnp.concatenate([attr_grad.reshape(-1), jnp.pad(camera, (0, 128 - 12))])
    gathered = lax.all_gather(payload.reshape(-1, 128), "views", axis=0, tiled=False)
    gathered = gathered.reshape(gathered.shape[0], -1)
    view_grads = gathered[:, : 9 * owned].reshape(-1, 9, owned)
    view_cameras = gathered[:, 9 * owned : 9 * owned + 12]

    def pull(view_camera, grad):
        ignored, pullback = jax.vjp(
            partial(project, camera=view_camera, center_x=center_x, center_y=center_y),
            gaussians,
        )
        return pullback(grad)[0]

    total = jnp.sum(jax.vmap(pull)(view_cameras, view_grads), axis=0)
    new_values, first_new, second_new = adam_step(
        gaussians, moment_one, moment_two, total, learn_rates
    )
    return (images[None].astype(jnp.bfloat16), new_values, first_new, second_new)


def solution(mesh):
    return jax.shard_map(
        body,
        mesh=mesh,
        in_specs=(
            P(None, "tiles"),
            P(None, "tiles"),
            P(None, "tiles"),
            P(),
            P(),
            P("views"),
            P("views", "tiles", None, None),
            P("views", "tiles", None),
            P("views", "tiles"),
            P("views", "tiles", None, None),
            P(),
        ),
        out_specs=(
            P("views", "tiles", None, None),
            P(None, "tiles"),
            P(None, "tiles"),
            P(None, "tiles"),
        ),
        check_vma=False,
    )
```

```python
from functools import partial

import jax
import jax.numpy as jnp
from jax import lax
from jax.experimental import pallas as pl
from jax.experimental.pallas import tpu as pltpu
from jax.sharding import PartitionSpec as P

TILE_SIDE = 32
PIXELS = 1024
TILE_ROWS = 8
LIST = 1024
BLOCK = 128
KB = 128


focal_length = 400.0
precise = lax.Precision.HIGHEST
decay_one = 0.9
decay_two = 0.999
adam_epsilon = 1e-08


def sh_basis(direction):
    dir_x, dir_y, dir_z = (direction[0], direction[1], direction[2])
    sq_x, sq_y, sq_z = (dir_x * dir_x, dir_y * dir_y, dir_z * dir_z)
    terms = [
        0.28209479177387814 * jnp.ones_like(dir_x),
        -0.4886025119029199 * dir_y,
        0.4886025119029199 * dir_z,
        -0.4886025119029199 * dir_x,
        1.0925484305920792 * dir_x * dir_y,
        -1.0925484305920792 * dir_y * dir_z,
        0.31539156525252005 * (2.0 * sq_z - sq_x - sq_y),
        -1.0925484305920792 * dir_x * dir_z,
        0.5462742152960396 * (sq_x - sq_y),
        -0.5900435899266435 * dir_y * (3.0 * sq_x - sq_y),
        2.890611442640554 * dir_x * dir_y * dir_z,
        -0.4570457994644658 * dir_y * (4.0 * sq_z - sq_x - sq_y),
        0.3731763325901154 * dir_z * (2.0 * sq_z - 3.0 * sq_x - 3.0 * sq_y),
        -0.4570457994644658 * dir_x * (4.0 * sq_z - sq_x - sq_y),
        1.445305721320277 * dir_z * (sq_x - sq_y),
        -0.5900435899266435 * dir_x * (sq_x - 3.0 * sq_y),
    ]
    return jnp.stack(terms)


def quat_rotation(quat):
    length = jnp.sqrt(jnp.sum(quat * quat, axis=0))
    quat_w, quat_x, quat_y, quat_z = (
        quat[0] / length,
        quat[1] / length,
        quat[2] / length,
        quat[3] / length,
    )
    rows = [
        [
            1.0 - 2.0 * (quat_y * quat_y + quat_z * quat_z),
            2.0 * (quat_x * quat_y - quat_w * quat_z),
            2.0 * (quat_x * quat_z + quat_w * quat_y),
        ],
        [
            2.0 * (quat_x * quat_y + quat_w * quat_z),
            1.0 - 2.0 * (quat_x * quat_x + quat_z * quat_z),
            2.0 * (quat_y * quat_z - quat_w * quat_x),
        ],
        [
            2.0 * (quat_x * quat_z - quat_w * quat_y),
            2.0 * (quat_y * quat_z + quat_w * quat_x),
            1.0 - 2.0 * (quat_x * quat_x + quat_y * quat_y),
        ],
    ]
    return jnp.stack([jnp.stack(entries) for entries in rows])


def project(params, camera, center_x, center_y):
    means = params[0:3]
    rotate = camera[0:9].reshape(3, 3)
    shift = camera[9:12]
    view_pos = jnp.dot(rotate, means, precision=precise) + shift[:, None]
    inv_depth = 1.0 / view_pos[2]
    image_x = focal_length * view_pos[0] * inv_depth + center_x
    image_y = focal_length * view_pos[1] * inv_depth + center_y
    scales = jnp.exp(params[3:6])
    local_axes = quat_rotation(params[6:10]) * scales[None, :, :]
    world_axes = jnp.einsum("ik,kjg->ijg", rotate, local_axes, precision=precise)
    proj_x = (
        focal_length * inv_depth * world_axes[0]
        - focal_length * view_pos[0] * inv_depth * inv_depth * world_axes[2]
    )
    proj_y = (
        focal_length * inv_depth * world_axes[1]
        - focal_length * view_pos[1] * inv_depth * inv_depth * world_axes[2]
    )
    cov_xx = jnp.sum(proj_x * proj_x, axis=0) + 0.3
    cov_xy = jnp.sum(proj_x * proj_y, axis=0)
    cov_yy = jnp.sum(proj_y * proj_y, axis=0) + 0.3
    determ = cov_xx * cov_yy - cov_xy * cov_xy
    opacity = 0.99 * jax.nn.sigmoid(params[10])
    center = -jnp.dot(rotate.T, shift, precision=precise)
    offset = means - center[:, None]
    direction = offset / jnp.sqrt(jnp.sum(offset * offset, axis=0))
    basis = sh_basis(direction)
    coeffs = params[11:59].reshape(16, 3, -1)
    colors = 0.5 + jnp.sum(basis[:, None, :] * coeffs, axis=0)
    head = jnp.stack(
        [image_x, image_y, cov_yy / determ, -cov_xy / determ, cov_xx / determ, opacity]
    )
    return jnp.concatenate([head, colors], axis=0)


def pixel_grid(tile, tile_cols):
    offsets = jnp.arange(PIXELS)
    pixel_x = (tile % tile_cols * TILE_SIDE + offsets % TILE_SIDE).astype(jnp.float32) + 0.5
    pixel_y = (tile // tile_cols * TILE_SIDE + offsets // TILE_SIDE).astype(jnp.float32) + 0.5
    return (pixel_x, pixel_y)


def block_terms(entry, count, pixel_x, pixel_y, index):
    start = index * BLOCK
    piece = lax.dynamic_slice_in_dim(entry, start, BLOCK, 1)
    live = (start + jnp.arange(BLOCK) < count)[None, :]
    delta_x = pixel_x[:, None] - piece[0][None, :]
    delta_y = pixel_y[:, None] - piece[1][None, :]
    power = -0.5 * (
        piece[2] * delta_x * delta_x
        + 2.0 * piece[3] * delta_x * delta_y
        + piece[4] * delta_y * delta_y
    )
    falloff = jnp.exp(power)
    alpha = jnp.where(live, piece[5][None, :] * falloff, 0.0)
    log_keep = jnp.log1p(-alpha)
    return (start, piece, live, delta_x, delta_y, falloff, alpha, log_keep)


def tile_pass(entry, count, pixel_x, pixel_y, target, background):
    blocks = (count + BLOCK - 1) // BLOCK

    def forward(index, carry):
        color, log_total = carry
        start, piece, live, delta_x, delta_y, falloff, alpha, log_keep = block_terms(
            entry, count, pixel_x, pixel_y, index
        )
        weight = jnp.exp(log_total[:, None] + jnp.cumsum(log_keep, axis=1) - log_keep) * alpha
        color = color + lax.dot_general(
            piece[6:9], weight, (((1,), (1,)), ((), ())), precision=precise
        )
        return (color, log_total + jnp.sum(log_keep, axis=1))

    zeros_pix = jnp.zeros((PIXELS,), jnp.float32)
    color, log_total = lax.fori_loop(
        0, blocks, forward, (jnp.zeros((3, PIXELS), jnp.float32), zeros_pix)
    )
    image = color + jnp.exp(log_total)[None, :] * background[:, None]
    resid = image - target
    dot_total = jnp.sum(image * resid, axis=0)

    def backward(index, carry):
        grads, log_before, prefix = carry
        start, piece, live, delta_x, delta_y, falloff, alpha, log_keep = block_terms(
            entry, count, pixel_x, pixel_y, index
        )
        trans = jnp.exp(log_before[:, None] + jnp.cumsum(log_keep, axis=1) - log_keep)
        weight = trans * alpha
        along = lax.dot_general(resid, piece[6:9], (((0,), (0,)), ((), ())), precision=precise)
        running = prefix[:, None] + jnp.cumsum(weight * along, axis=1)
        d_alpha = jnp.where(
            live, trans * along - (dot_total[:, None] - running) / (1.0 - alpha), 0.0
        )
        d_power = d_alpha * alpha
        sum_x = jnp.sum(d_power * delta_x, axis=0)
        sum_y = jnp.sum(d_power * delta_y, axis=0)
        head = jnp.stack(
            [
                piece[2] * sum_x + piece[3] * sum_y,
                piece[3] * sum_x + piece[4] * sum_y,
                -0.5 * jnp.sum(d_power * delta_x * delta_x, axis=0),
                -jnp.sum(d_power * delta_x * delta_y, axis=0),
                -0.5 * jnp.sum(d_power * delta_y * delta_y, axis=0),
                jnp.sum(d_alpha * falloff, axis=0),
            ]
        )
        color_grad = jnp.dot(resid, weight, precision=precise)
        block_grad = jnp.concatenate([head, color_grad], axis=0)
        grads = lax.dynamic_update_slice_in_dim(grads, block_grad, start, 1)
        return (grads, log_before + jnp.sum(log_keep, axis=1), running[:, -1])

    start_grads = jnp.zeros((9, LIST), jnp.float32)
    grads, ignored, unused = lax.fori_loop(0, blocks, backward, (start_grads, zeros_pix, zeros_pix))
    return (image, grads)


def split_cumsum(x, upper):
    high = x.astype(jnp.bfloat16)
    rest = x - high.astype(jnp.float32)
    middle = rest.astype(jnp.bfloat16)
    low = (rest - middle.astype(jnp.float32)).astype(jnp.bfloat16)
    total = jnp.dot(high, upper, preferred_element_type=jnp.float32)
    total = total + jnp.dot(middle, upper, preferred_element_type=jnp.float32)
    return total + jnp.dot(low, upper, preferred_element_type=jnp.float32)


def render_kernel(
    counts_ref, tiles_ref, entry_ref, target_ref, bg_ref, image_ref, sums_ref, trans_ref, fall_ref, *, tile_cols
):
    t = pl.program_id(0)
    count = counts_ref[t]
    tile = tiles_ref[t]
    blocks = (count + KB - 1) // KB
    sums_ref[...] = jnp.zeros(sums_ref.shape, jnp.float32)
    row = lax.broadcasted_iota(jnp.int32, (KB, KB), 0)
    col = lax.broadcasted_iota(jnp.int32, (KB, KB), 1)
    upper = (row <= col).astype(jnp.bfloat16)
    lane = lax.broadcasted_iota(jnp.int32, (1, KB), 1)
    pixel = lax.broadcasted_iota(jnp.int32, (PIXELS, KB), 0)
    pix_x = ((tile % tile_cols) * TILE_SIDE + pixel % TILE_SIDE).astype(jnp.float32) + 0.5
    pix_y = ((tile // tile_cols) * TILE_SIDE + pixel // TILE_SIDE).astype(jnp.float32) + 0.5

    def geometry(index):
        start = pl.multiple_of(index * KB, KB)
        blk = entry_ref[:, pl.ds(start, KB)]
        live = (start + lane) < count
        return start, blk, live, pix_x - blk[0:1], pix_y - blk[1:2]

    def forward(i, carry):
        log_total, red, green, blue = carry
        start, blk, live, dx, dy = geometry(i)
        power = -0.5 * (blk[2:3] * dx * dx + 2.0 * blk[3:4] * dx * dy + blk[4:5] * dy * dy)
        falloff = jnp.exp(power)
        alpha = jnp.where(live, blk[5:6] * falloff, 0.0)
        log_keep = jnp.log1p(-alpha)
        cum = split_cumsum(log_keep, upper)
        trans = jnp.exp(log_total + cum - log_keep)
        weight = trans * alpha
        trans_ref[:, pl.ds(start, KB)] = trans
        fall_ref[:, pl.ds(start, KB)] = falloff
        return (
            log_total + cum[:, KB - 1 : KB],
            red + weight * blk[8:9],
            green + weight * blk[9:10],
            blue + weight * blk[10:11],
        )

    zeros = jnp.zeros((PIXELS, KB), jnp.float32)
    log_total, red, green, blue = lax.fori_loop(
        0, blocks, forward, (jnp.zeros((PIXELS, 1), jnp.float32), zeros, zeros, zeros)
    )
    lane8 = lax.broadcasted_iota(jnp.int32, (1, 8), 1)
    color = (
        jnp.where(lane8 == 0, jnp.sum(red, axis=1, keepdims=True), 0.0)
        + jnp.where(lane8 == 1, jnp.sum(green, axis=1, keepdims=True), 0.0)
        + jnp.where(lane8 == 2, jnp.sum(blue, axis=1, keepdims=True), 0.0)
    )
    image = color + jnp.exp(log_total) * bg_ref[...]
    image_ref[...] = image
    resid = image - target_ref[...]
    dot_total = jnp.sum(image * resid, axis=1, keepdims=True)
    resid_r, resid_g, resid_b = resid[:, 0:1], resid[:, 1:2], resid[:, 2:3]

    def backward(i, prefix):
        start, blk, live, dx, dy = geometry(i)
        trans = trans_ref[:, pl.ds(start, KB)]
        falloff = fall_ref[:, pl.ds(start, KB)]
        alpha = jnp.where(live, blk[5:6] * falloff, 0.0)
        weight = trans * alpha
        along = resid_r * blk[8:9] + resid_g * blk[9:10] + resid_b * blk[10:11]
        running = prefix + split_cumsum(weight * along, upper)
        d_alpha = jnp.where(live, trans * along - (dot_total - running) / (1.0 - alpha), 0.0)
        d_power = d_alpha * alpha
        x_term = d_power * dx
        y_term = d_power * dy
        parts = [
            x_term,
            y_term,
            x_term * dx,
            x_term * dy,
            y_term * dy,
            d_alpha * falloff,
            weight * resid_r,
            weight * resid_g,
            weight * resid_b,
        ]
        for r, part in enumerate(parts):
            sums_ref[r : r + 1, pl.ds(start, KB)] += jnp.sum(part, axis=0, keepdims=True)
        return running[:, KB - 1 : KB]

    lax.fori_loop(0, blocks, backward, jnp.zeros((PIXELS, 1), jnp.float32))


def render_tiles(entry16, counts, tiles, target8, bg8, tile_cols):
    n = entry16.shape[0]
    return pl.pallas_call(
        partial(render_kernel, tile_cols=tile_cols),
        grid=(n,),
        in_specs=[
            pl.BlockSpec(memory_space=pltpu.SMEM),
            pl.BlockSpec(memory_space=pltpu.SMEM),
            pl.BlockSpec((None, 16, LIST), lambda t: (t, 0, 0)),
            pl.BlockSpec((None, PIXELS, 8), lambda t: (t, 0, 0)),
            pl.BlockSpec((1, 8), lambda t: (0, 0)),
        ],
        out_specs=[
            pl.BlockSpec((None, PIXELS, 8), lambda t: (t, 0, 0)),
            pl.BlockSpec((None, 16, LIST), lambda t: (t, 0, 0)),
        ],
        out_shape=[
            jax.ShapeDtypeStruct((n, PIXELS, 8), jnp.float32),
            jax.ShapeDtypeStruct((n, 16, LIST), jnp.float32),
        ],
        scratch_shapes=[
            pltpu.VMEM((PIXELS, LIST), jnp.float32),
            pltpu.VMEM((PIXELS, LIST), jnp.float32),
        ],
    )(counts, tiles, entry16, target8, bg8)


def select_rows(values, chosen, contract):
    high = lax.reduce_precision(values, exponent_bits=8, mantissa_bits=7)
    rest = values - high
    middle = lax.reduce_precision(rest, exponent_bits=8, mantissa_bits=7)
    low = rest - middle
    pieces = jnp.concatenate([high, middle, low], axis=0).astype(jnp.bfloat16)
    out = lax.dot_general(
        pieces, chosen, (((1,), (contract,)), ((), ())), preferred_element_type=jnp.float32
    )
    rows = values.shape[0]
    return (out[:rows] + out[rows : 2 * rows]) + out[2 * rows :]


def adam_step(values, first, second, grad, rates):
    first_new = decay_one * first + (1.0 - decay_one) * grad
    second_new = decay_two * second + (1.0 - decay_two) * grad * grad
    return (
        values - rates[:, None] * first_new / (jnp.sqrt(second_new) + adam_epsilon),
        first_new,
        second_new,
    )


def body(
    gaussians,
    moment_one,
    moment_two,
    learn_rates,
    cameras,
    camera_ids,
    list_owner,
    list_index,
    list_length,
    targets,
    background,
):
    peers = lax.axis_size("tiles")
    tiles_here = list_index.shape[1]
    entries = tiles_here * LIST
    owned = gaussians.shape[1]
    capacity = 2 * entries // peers
    tile_cols = tiles_here * peers // TILE_ROWS
    center_x = 0.5 * TILE_SIDE * tile_cols
    center_y = 0.5 * TILE_SIDE * TILE_ROWS
    camera = cameras[camera_ids[0]]
    attrs = project(gaussians, camera, center_x, center_y)
    owner_flat = list_owner.reshape(-1)
    index_flat = list_index.reshape(-1)
    earlier = jnp.arange(entries)[None, :] < jnp.arange(entries)[:, None]
    same = owner_flat[:, None] == owner_flat[None, :]
    rank = jnp.sum((same & earlier).astype(jnp.int32), axis=1)
    slot = owner_flat * capacity + rank
    placed = (slot[:, None] == jnp.arange(peers * capacity)[None, :]).astype(jnp.bfloat16)
    asked_for = (
        jnp.round(select_rows(index_flat.astype(jnp.float32)[None], placed, 0))
        .astype(jnp.int32)
        .reshape(peers, capacity)
    )
    asked = lax.all_to_all(asked_for, "tiles", split_axis=0, concat_axis=0, tiled=True)
    chosen = (asked.reshape(-1)[:, None] == jnp.arange(owned)[None, :]).astype(jnp.bfloat16)
    served = select_rows(attrs, chosen, 1).reshape(9, peers, capacity)
    returned = lax.all_to_all(served, "tiles", split_axis=1, concat_axis=1, tiled=True)
    entry_attrs = select_rows(returned.reshape(9, peers * capacity), placed, 1).reshape(
        9, tiles_here, LIST
    )
    first_tile = lax.axis_index("tiles") * tiles_here

    colors_pad = jnp.zeros((5, tiles_here, LIST), jnp.float32)
    entry16 = jnp.moveaxis(
        jnp.concatenate([entry_attrs[0:6], colors_pad[0:2], entry_attrs[6:9], colors_pad], axis=0), 1, 0
    )
    target8 = jnp.pad(
        jnp.swapaxes(targets[0].astype(jnp.float32), 1, 2), ((0, 0), (0, 0), (0, 5))
    )
    background8 = jnp.pad(background, (0, 5))[None]
    tile_ids = first_tile + jnp.arange(tiles_here, dtype=jnp.int32)
    image8, sums = render_tiles(entry16, list_length[0], tile_ids, target8, background8, tile_cols)
    images = jnp.swapaxes(image8[:, :, 0:3], 1, 2)
    sums = jnp.moveaxis(sums, 1, 0).reshape(16, entries)
    flat = entry_attrs.reshape(9, entries)
    flat_grads = jnp.stack(
        [
            flat[2] * sums[0] + flat[3] * sums[1],
            flat[3] * sums[0] + flat[4] * sums[1],
            -0.5 * sums[2],
            -sums[3],
            -0.5 * sums[4],
            sums[5],
            sums[6],
            sums[7],
            sums[8],
        ]
    )
    grad_send = select_rows(flat_grads, placed, 0).reshape(9, peers, capacity)
    grad_back = lax.all_to_all(grad_send, "tiles", split_axis=1, concat_axis=1, tiled=True)
    attr_grad = select_rows(grad_back.reshape(9, peers * capacity), chosen, 0)
    payload = jnp.concatenate([attr_grad.reshape(-1), jnp.pad(camera, (0, 128 - 12))])
    gathered = lax.all_gather(payload.reshape(-1, 128), "views", axis=0, tiled=False)
    gathered = gathered.reshape(gathered.shape[0], -1)
    view_grads = gathered[:, : 9 * owned].reshape(-1, 9, owned)
    view_cameras = gathered[:, 9 * owned : 9 * owned + 12]

    def pull(view_camera, grad):
        ignored, pullback = jax.vjp(
            partial(project, camera=view_camera, center_x=center_x, center_y=center_y),
            gaussians,
        )
        return pullback(grad)[0]

    total = jnp.sum(jax.vmap(pull)(view_cameras, view_grads), axis=0)
    new_values, first_new, second_new = adam_step(
        gaussians, moment_one, moment_two, total, learn_rates
    )
    return (images[None].astype(jnp.bfloat16), new_values, first_new, second_new)


def solution(mesh):
    return jax.shard_map(
        body,
        mesh=mesh,
        in_specs=(
            P(None, "tiles"),
            P(None, "tiles"),
            P(None, "tiles"),
            P(),
            P(),
            P("views"),
            P("views", "tiles", None, None),
            P("views", "tiles", None),
            P("views", "tiles"),
            P("views", "tiles", None, None),
            P(),
        ),
        out_specs=(
            P("views", "tiles", None, None),
            P(None, "tiles"),
            P(None, "tiles"),
            P(None, "tiles"),
        ),
        check_vma=False,
    )
```

```python
from functools import partial

import jax
import jax.numpy as jnp
from jax import lax
from jax.experimental import pallas as pl
from jax.experimental.pallas import tpu as pltpu
from jax.sharding import PartitionSpec as P

TILE_SIDE = 32
PIXELS = 1024
TILE_ROWS = 8
LIST = 1024
BLOCK = 128
KB = 128


focal_length = 400.0
precise = lax.Precision.HIGHEST
decay_one = 0.9
decay_two = 0.999
adam_epsilon = 1e-08


def sh_basis(direction):
    dir_x, dir_y, dir_z = (direction[0], direction[1], direction[2])
    sq_x, sq_y, sq_z = (dir_x * dir_x, dir_y * dir_y, dir_z * dir_z)
    terms = [
        0.28209479177387814 * jnp.ones_like(dir_x),
        -0.4886025119029199 * dir_y,
        0.4886025119029199 * dir_z,
        -0.4886025119029199 * dir_x,
        1.0925484305920792 * dir_x * dir_y,
        -1.0925484305920792 * dir_y * dir_z,
        0.31539156525252005 * (2.0 * sq_z - sq_x - sq_y),
        -1.0925484305920792 * dir_x * dir_z,
        0.5462742152960396 * (sq_x - sq_y),
        -0.5900435899266435 * dir_y * (3.0 * sq_x - sq_y),
        2.890611442640554 * dir_x * dir_y * dir_z,
        -0.4570457994644658 * dir_y * (4.0 * sq_z - sq_x - sq_y),
        0.3731763325901154 * dir_z * (2.0 * sq_z - 3.0 * sq_x - 3.0 * sq_y),
        -0.4570457994644658 * dir_x * (4.0 * sq_z - sq_x - sq_y),
        1.445305721320277 * dir_z * (sq_x - sq_y),
        -0.5900435899266435 * dir_x * (sq_x - 3.0 * sq_y),
    ]
    return jnp.stack(terms)


def quat_rotation(quat):
    length = jnp.sqrt(jnp.sum(quat * quat, axis=0))
    quat_w, quat_x, quat_y, quat_z = (
        quat[0] / length,
        quat[1] / length,
        quat[2] / length,
        quat[3] / length,
    )
    rows = [
        [
            1.0 - 2.0 * (quat_y * quat_y + quat_z * quat_z),
            2.0 * (quat_x * quat_y - quat_w * quat_z),
            2.0 * (quat_x * quat_z + quat_w * quat_y),
        ],
        [
            2.0 * (quat_x * quat_y + quat_w * quat_z),
            1.0 - 2.0 * (quat_x * quat_x + quat_z * quat_z),
            2.0 * (quat_y * quat_z - quat_w * quat_x),
        ],
        [
            2.0 * (quat_x * quat_z - quat_w * quat_y),
            2.0 * (quat_y * quat_z + quat_w * quat_x),
            1.0 - 2.0 * (quat_x * quat_x + quat_y * quat_y),
        ],
    ]
    return jnp.stack([jnp.stack(entries) for entries in rows])


def project(params, camera, center_x, center_y):
    means = params[0:3]
    rotate = camera[0:9].reshape(3, 3)
    shift = camera[9:12]
    view_pos = jnp.dot(rotate, means, precision=precise) + shift[:, None]
    inv_depth = 1.0 / view_pos[2]
    image_x = focal_length * view_pos[0] * inv_depth + center_x
    image_y = focal_length * view_pos[1] * inv_depth + center_y
    scales = jnp.exp(params[3:6])
    local_axes = quat_rotation(params[6:10]) * scales[None, :, :]
    world_axes = jnp.einsum("ik,kjg->ijg", rotate, local_axes, precision=precise)
    proj_x = (
        focal_length * inv_depth * world_axes[0]
        - focal_length * view_pos[0] * inv_depth * inv_depth * world_axes[2]
    )
    proj_y = (
        focal_length * inv_depth * world_axes[1]
        - focal_length * view_pos[1] * inv_depth * inv_depth * world_axes[2]
    )
    cov_xx = jnp.sum(proj_x * proj_x, axis=0) + 0.3
    cov_xy = jnp.sum(proj_x * proj_y, axis=0)
    cov_yy = jnp.sum(proj_y * proj_y, axis=0) + 0.3
    determ = cov_xx * cov_yy - cov_xy * cov_xy
    opacity = 0.99 * jax.nn.sigmoid(params[10])
    center = -jnp.dot(rotate.T, shift, precision=precise)
    offset = means - center[:, None]
    direction = offset / jnp.sqrt(jnp.sum(offset * offset, axis=0))
    basis = sh_basis(direction)
    coeffs = params[11:59].reshape(16, 3, -1)
    colors = 0.5 + jnp.sum(basis[:, None, :] * coeffs, axis=0)
    head = jnp.stack(
        [image_x, image_y, cov_yy / determ, -cov_xy / determ, cov_xx / determ, opacity]
    )
    return jnp.concatenate([head, colors], axis=0)


def pixel_grid(tile, tile_cols):
    offsets = jnp.arange(PIXELS)
    pixel_x = (tile % tile_cols * TILE_SIDE + offsets % TILE_SIDE).astype(jnp.float32) + 0.5
    pixel_y = (tile // tile_cols * TILE_SIDE + offsets // TILE_SIDE).astype(jnp.float32) + 0.5
    return (pixel_x, pixel_y)


def block_terms(entry, count, pixel_x, pixel_y, index):
    start = index * BLOCK
    piece = lax.dynamic_slice_in_dim(entry, start, BLOCK, 1)
    live = (start + jnp.arange(BLOCK) < count)[None, :]
    delta_x = pixel_x[:, None] - piece[0][None, :]
    delta_y = pixel_y[:, None] - piece[1][None, :]
    power = -0.5 * (
        piece[2] * delta_x * delta_x
        + 2.0 * piece[3] * delta_x * delta_y
        + piece[4] * delta_y * delta_y
    )
    falloff = jnp.exp(power)
    alpha = jnp.where(live, piece[5][None, :] * falloff, 0.0)
    log_keep = jnp.log1p(-alpha)
    return (start, piece, live, delta_x, delta_y, falloff, alpha, log_keep)


def tile_pass(entry, count, pixel_x, pixel_y, target, background):
    blocks = (count + BLOCK - 1) // BLOCK

    def forward(index, carry):
        color, log_total = carry
        start, piece, live, delta_x, delta_y, falloff, alpha, log_keep = block_terms(
            entry, count, pixel_x, pixel_y, index
        )
        weight = jnp.exp(log_total[:, None] + jnp.cumsum(log_keep, axis=1) - log_keep) * alpha
        color = color + lax.dot_general(
            piece[6:9], weight, (((1,), (1,)), ((), ())), precision=precise
        )
        return (color, log_total + jnp.sum(log_keep, axis=1))

    zeros_pix = jnp.zeros((PIXELS,), jnp.float32)
    color, log_total = lax.fori_loop(
        0, blocks, forward, (jnp.zeros((3, PIXELS), jnp.float32), zeros_pix)
    )
    image = color + jnp.exp(log_total)[None, :] * background[:, None]
    resid = image - target
    dot_total = jnp.sum(image * resid, axis=0)

    def backward(index, carry):
        grads, log_before, prefix = carry
        start, piece, live, delta_x, delta_y, falloff, alpha, log_keep = block_terms(
            entry, count, pixel_x, pixel_y, index
        )
        trans = jnp.exp(log_before[:, None] + jnp.cumsum(log_keep, axis=1) - log_keep)
        weight = trans * alpha
        along = lax.dot_general(resid, piece[6:9], (((0,), (0,)), ((), ())), precision=precise)
        running = prefix[:, None] + jnp.cumsum(weight * along, axis=1)
        d_alpha = jnp.where(
            live, trans * along - (dot_total[:, None] - running) / (1.0 - alpha), 0.0
        )
        d_power = d_alpha * alpha
        sum_x = jnp.sum(d_power * delta_x, axis=0)
        sum_y = jnp.sum(d_power * delta_y, axis=0)
        head = jnp.stack(
            [
                piece[2] * sum_x + piece[3] * sum_y,
                piece[3] * sum_x + piece[4] * sum_y,
                -0.5 * jnp.sum(d_power * delta_x * delta_x, axis=0),
                -jnp.sum(d_power * delta_x * delta_y, axis=0),
                -0.5 * jnp.sum(d_power * delta_y * delta_y, axis=0),
                jnp.sum(d_alpha * falloff, axis=0),
            ]
        )
        color_grad = jnp.dot(resid, weight, precision=precise)
        block_grad = jnp.concatenate([head, color_grad], axis=0)
        grads = lax.dynamic_update_slice_in_dim(grads, block_grad, start, 1)
        return (grads, log_before + jnp.sum(log_keep, axis=1), running[:, -1])

    start_grads = jnp.zeros((9, LIST), jnp.float32)
    grads, ignored, unused = lax.fori_loop(0, blocks, backward, (start_grads, zeros_pix, zeros_pix))
    return (image, grads)


def split_cumsum(x, upper):
    high = x.astype(jnp.bfloat16)
    rest = x - high.astype(jnp.float32)
    middle = rest.astype(jnp.bfloat16)
    low = (rest - middle.astype(jnp.float32)).astype(jnp.bfloat16)
    total = jnp.dot(high, upper, preferred_element_type=jnp.float32)
    total = total + jnp.dot(middle, upper, preferred_element_type=jnp.float32)
    return total + jnp.dot(low, upper, preferred_element_type=jnp.float32)


def render_kernel(
    counts_ref, tiles_ref, entry_ref, target_ref, bg_ref, image_ref, sums_ref, trans_ref, fall_ref, *, tile_cols
):
    t = pl.program_id(0)
    count = counts_ref[t]
    tile = tiles_ref[t]
    blocks = (count + KB - 1) // KB
    sums_ref[...] = jnp.zeros(sums_ref.shape, jnp.float32)
    row = lax.broadcasted_iota(jnp.int32, (KB, KB), 0)
    col = lax.broadcasted_iota(jnp.int32, (KB, KB), 1)
    upper = (row <= col).astype(jnp.bfloat16)
    lane = lax.broadcasted_iota(jnp.int32, (1, KB), 1)
    pixel = lax.broadcasted_iota(jnp.int32, (PIXELS, KB), 0)
    pix_x = ((tile % tile_cols) * TILE_SIDE + pixel % TILE_SIDE).astype(jnp.float32) + 0.5
    pix_y = ((tile // tile_cols) * TILE_SIDE + pixel // TILE_SIDE).astype(jnp.float32) + 0.5

    def geometry(index):
        start = pl.multiple_of(index * KB, KB)
        blk = entry_ref[:, pl.ds(start, KB)]
        live = (start + lane) < count
        return start, blk, live, pix_x - blk[0:1], pix_y - blk[1:2]

    def forward(i, carry):
        log_total, red, green, blue = carry
        start, blk, live, dx, dy = geometry(i)
        power = -0.5 * (blk[2:3] * dx * dx + 2.0 * blk[3:4] * dx * dy + blk[4:5] * dy * dy)
        falloff = jnp.exp(power)
        alpha = jnp.where(live, blk[5:6] * falloff, 0.0)
        log_keep = jnp.log1p(-alpha)
        cum = split_cumsum(log_keep, upper)
        trans = jnp.exp(log_total + cum - log_keep)
        weight = trans * alpha
        trans_ref[:, pl.ds(start, KB)] = trans
        fall_ref[:, pl.ds(start, KB)] = falloff
        return (
            log_total + cum[:, KB - 1 : KB],
            red + weight * blk[8:9],
            green + weight * blk[9:10],
            blue + weight * blk[10:11],
        )

    zeros = jnp.zeros((PIXELS, KB), jnp.float32)
    log_total, red, green, blue = lax.fori_loop(
        0, blocks, forward, (jnp.zeros((PIXELS, 1), jnp.float32), zeros, zeros, zeros)
    )
    lane8 = lax.broadcasted_iota(jnp.int32, (1, 8), 1)
    color = (
        jnp.where(lane8 == 0, jnp.sum(red, axis=1, keepdims=True), 0.0)
        + jnp.where(lane8 == 1, jnp.sum(green, axis=1, keepdims=True), 0.0)
        + jnp.where(lane8 == 2, jnp.sum(blue, axis=1, keepdims=True), 0.0)
    )
    image = color + jnp.exp(log_total) * bg_ref[...]
    image_ref[...] = image
    resid = image - target_ref[...]
    dot_total = jnp.sum(image * resid, axis=1, keepdims=True)
    resid_r, resid_g, resid_b = resid[:, 0:1], resid[:, 1:2], resid[:, 2:3]

    def backward(i, prefix):
        start, blk, live, dx, dy = geometry(i)
        trans = trans_ref[:, pl.ds(start, KB)]
        falloff = fall_ref[:, pl.ds(start, KB)]
        alpha = jnp.where(live, blk[5:6] * falloff, 0.0)
        weight = trans * alpha
        along = resid_r * blk[8:9] + resid_g * blk[9:10] + resid_b * blk[10:11]
        running = prefix + split_cumsum(weight * along, upper)
        d_alpha = jnp.where(live, trans * along - (dot_total - running) / (1.0 - alpha), 0.0)
        d_power = d_alpha * alpha
        x_term = d_power * dx
        y_term = d_power * dy
        parts = [
            x_term,
            y_term,
            x_term * dx,
            x_term * dy,
            y_term * dy,
            d_alpha * falloff,
            weight * resid_r,
            weight * resid_g,
            weight * resid_b,
        ]
        for r, part in enumerate(parts):
            sums_ref[r : r + 1, pl.ds(start, KB)] += jnp.sum(part, axis=0, keepdims=True)
        return running[:, KB - 1 : KB]

    lax.fori_loop(0, blocks, backward, jnp.zeros((PIXELS, 1), jnp.float32))


def render_tiles(entry16, counts, tiles, target8, bg8, tile_cols):
    n = entry16.shape[0]
    return pl.pallas_call(
        partial(render_kernel, tile_cols=tile_cols),
        grid=(n,),
        in_specs=[
            pl.BlockSpec(memory_space=pltpu.SMEM),
            pl.BlockSpec(memory_space=pltpu.SMEM),
            pl.BlockSpec((None, 16, LIST), lambda t: (t, 0, 0)),
            pl.BlockSpec((None, PIXELS, 8), lambda t: (t, 0, 0)),
            pl.BlockSpec((1, 8), lambda t: (0, 0)),
        ],
        out_specs=[
            pl.BlockSpec((None, PIXELS, 8), lambda t: (t, 0, 0)),
            pl.BlockSpec((None, 16, LIST), lambda t: (t, 0, 0)),
        ],
        out_shape=[
            jax.ShapeDtypeStruct((n, PIXELS, 8), jnp.float32),
            jax.ShapeDtypeStruct((n, 16, LIST), jnp.float32),
        ],
        scratch_shapes=[
            pltpu.VMEM((PIXELS, LIST), jnp.float32),
            pltpu.VMEM((PIXELS, LIST), jnp.float32),
        ],
    )(counts, tiles, entry16, target8, bg8)


def select_rows(values, chosen, contract):
    high = lax.reduce_precision(values, exponent_bits=8, mantissa_bits=7)
    rest = values - high
    middle = lax.reduce_precision(rest, exponent_bits=8, mantissa_bits=7)
    low = rest - middle
    pieces = jnp.concatenate([high, middle, low], axis=0).astype(jnp.bfloat16)
    out = lax.dot_general(
        pieces, chosen, (((1,), (contract,)), ((), ())), preferred_element_type=jnp.float32
    )
    rows = values.shape[0]
    return (out[:rows] + out[rows : 2 * rows]) + out[2 * rows :]


def adam_step(values, first, second, grad, rates):
    first_new = decay_one * first + (1.0 - decay_one) * grad
    second_new = decay_two * second + (1.0 - decay_two) * grad * grad
    return (
        values - rates[:, None] * first_new / (jnp.sqrt(second_new) + adam_epsilon),
        first_new,
        second_new,
    )


def body(
    gaussians,
    moment_one,
    moment_two,
    learn_rates,
    cameras,
    camera_ids,
    list_owner,
    list_index,
    list_length,
    targets,
    background,
):
    peers = lax.axis_size("tiles")
    tiles_here = list_index.shape[1]
    entries = tiles_here * LIST
    owned = gaussians.shape[1]
    capacity = 2 * entries // peers
    tile_cols = tiles_here * peers // TILE_ROWS
    center_x = 0.5 * TILE_SIDE * tile_cols
    center_y = 0.5 * TILE_SIDE * TILE_ROWS
    camera = cameras[camera_ids[0]]
    attrs = project(gaussians, camera, center_x, center_y)
    owner_flat = list_owner.reshape(-1)
    index_flat = list_index.reshape(-1)
    earlier = jnp.arange(entries)[None, :] < jnp.arange(entries)[:, None]
    same = owner_flat[:, None] == owner_flat[None, :]
    rank = jnp.sum((same & earlier).astype(jnp.int32), axis=1)
    slot = owner_flat * capacity + rank
    placed = (slot[:, None] == jnp.arange(peers * capacity)[None, :]).astype(jnp.bfloat16)
    asked_for = (
        jnp.round(select_rows(index_flat.astype(jnp.float32)[None], placed, 0))
        .astype(jnp.int32)
        .reshape(peers, capacity)
    )
    asked = lax.all_to_all(asked_for, "tiles", split_axis=0, concat_axis=0, tiled=True)
    chosen = (asked.reshape(-1)[:, None] == jnp.arange(owned)[None, :]).astype(jnp.bfloat16)
    served = select_rows(attrs, chosen, 1).reshape(9, peers, capacity)
    returned = lax.all_to_all(served, "tiles", split_axis=1, concat_axis=1, tiled=True)
    entry_attrs = select_rows(returned.reshape(9, peers * capacity), placed, 1).reshape(
        9, tiles_here, LIST
    )
    first_tile = lax.axis_index("tiles") * tiles_here

    colors_pad = jnp.zeros((5, tiles_here, LIST), jnp.float32)
    entry16 = jnp.moveaxis(
        jnp.concatenate([entry_attrs[0:6], colors_pad[0:2], entry_attrs[6:9], colors_pad], axis=0), 1, 0
    )
    target8 = jnp.pad(
        jnp.swapaxes(targets[0].astype(jnp.float32), 1, 2), ((0, 0), (0, 0), (0, 5))
    )
    background8 = jnp.pad(background, (0, 5))[None]
    tile_ids = first_tile + jnp.arange(tiles_here, dtype=jnp.int32)
    image8, sums = render_tiles(entry16, list_length[0], tile_ids, target8, background8, tile_cols)
    images = jnp.swapaxes(image8[:, :, 0:3], 1, 2)
    sums = jnp.moveaxis(sums, 1, 0).reshape(16, entries)
    flat = entry_attrs.reshape(9, entries)
    flat_grads = jnp.stack(
        [
            flat[2] * sums[0] + flat[3] * sums[1],
            flat[3] * sums[0] + flat[4] * sums[1],
            -0.5 * sums[2],
            -sums[3],
            -0.5 * sums[4],
            sums[5],
            sums[6],
            sums[7],
            sums[8],
        ]
    )
    grad_send = select_rows(flat_grads, placed, 0).reshape(9, peers, capacity)
    grad_back = lax.all_to_all(grad_send, "tiles", split_axis=1, concat_axis=1, tiled=True)
    attr_grad = select_rows(grad_back.reshape(9, peers * capacity), chosen, 0)
    payload = jnp.concatenate([attr_grad.reshape(-1), jnp.pad(camera, (0, 128 - 12))])
    views = lax.axis_size("views")
    view = lax.axis_index("views")
    shifted = [payload] + [
        lax.ppermute(payload, "views", [(i, (i + s) % views) for i in range(views)])
        for s in range(1, views)
    ]
    gathered = jnp.stack(shifted)[(view - jnp.arange(views)) % views]
    view_grads = gathered[:, : 9 * owned].reshape(-1, 9, owned)
    view_cameras = gathered[:, 9 * owned : 9 * owned + 12]

    def pull(view_camera, grad):
        ignored, pullback = jax.vjp(
            partial(project, camera=view_camera, center_x=center_x, center_y=center_y),
            gaussians,
        )
        return pullback(grad)[0]

    total = jnp.sum(jax.vmap(pull)(view_cameras, view_grads), axis=0)
    new_values, first_new, second_new = adam_step(
        gaussians, moment_one, moment_two, total, learn_rates
    )
    return (images[None].astype(jnp.bfloat16), new_values, first_new, second_new)


def solution(mesh):
    return jax.shard_map(
        body,
        mesh=mesh,
        in_specs=(
            P(None, "tiles"),
            P(None, "tiles"),
            P(None, "tiles"),
            P(),
            P(),
            P("views"),
            P("views", "tiles", None, None),
            P("views", "tiles", None),
            P("views", "tiles"),
            P("views", "tiles", None, None),
            P(),
        ),
        out_specs=(
            P("views", "tiles", None, None),
            P(None, "tiles"),
            P(None, "tiles"),
            P(None, "tiles"),
        ),
        check_vma=False,
    )
```

```python
from functools import partial

import jax
import jax.numpy as jnp
from jax import lax
from jax.experimental import pallas as pl
from jax.experimental.pallas import tpu as pltpu
from jax.sharding import PartitionSpec as P

TILE_SIDE = 32
PIXELS = 1024
TILE_ROWS = 8
LIST = 1024
BLOCK = 128
KB = 256


focal_length = 400.0
precise = lax.Precision.HIGHEST
decay_one = 0.9
decay_two = 0.999
adam_epsilon = 1e-08


def sh_basis(direction):
    dir_x, dir_y, dir_z = (direction[0], direction[1], direction[2])
    sq_x, sq_y, sq_z = (dir_x * dir_x, dir_y * dir_y, dir_z * dir_z)
    terms = [
        0.28209479177387814 * jnp.ones_like(dir_x),
        -0.4886025119029199 * dir_y,
        0.4886025119029199 * dir_z,
        -0.4886025119029199 * dir_x,
        1.0925484305920792 * dir_x * dir_y,
        -1.0925484305920792 * dir_y * dir_z,
        0.31539156525252005 * (2.0 * sq_z - sq_x - sq_y),
        -1.0925484305920792 * dir_x * dir_z,
        0.5462742152960396 * (sq_x - sq_y),
        -0.5900435899266435 * dir_y * (3.0 * sq_x - sq_y),
        2.890611442640554 * dir_x * dir_y * dir_z,
        -0.4570457994644658 * dir_y * (4.0 * sq_z - sq_x - sq_y),
        0.3731763325901154 * dir_z * (2.0 * sq_z - 3.0 * sq_x - 3.0 * sq_y),
        -0.4570457994644658 * dir_x * (4.0 * sq_z - sq_x - sq_y),
        1.445305721320277 * dir_z * (sq_x - sq_y),
        -0.5900435899266435 * dir_x * (sq_x - 3.0 * sq_y),
    ]
    return jnp.stack(terms)


def quat_rotation(quat):
    length = jnp.sqrt(jnp.sum(quat * quat, axis=0))
    quat_w, quat_x, quat_y, quat_z = (
        quat[0] / length,
        quat[1] / length,
        quat[2] / length,
        quat[3] / length,
    )
    rows = [
        [
            1.0 - 2.0 * (quat_y * quat_y + quat_z * quat_z),
            2.0 * (quat_x * quat_y - quat_w * quat_z),
            2.0 * (quat_x * quat_z + quat_w * quat_y),
        ],
        [
            2.0 * (quat_x * quat_y + quat_w * quat_z),
            1.0 - 2.0 * (quat_x * quat_x + quat_z * quat_z),
            2.0 * (quat_y * quat_z - quat_w * quat_x),
        ],
        [
            2.0 * (quat_x * quat_z - quat_w * quat_y),
            2.0 * (quat_y * quat_z + quat_w * quat_x),
            1.0 - 2.0 * (quat_x * quat_x + quat_y * quat_y),
        ],
    ]
    return jnp.stack([jnp.stack(entries) for entries in rows])


def project(params, camera, center_x, center_y):
    means = params[0:3]
    rotate = camera[0:9].reshape(3, 3)
    shift = camera[9:12]
    view_pos = jnp.dot(rotate, means, precision=precise) + shift[:, None]
    inv_depth = 1.0 / view_pos[2]
    image_x = focal_length * view_pos[0] * inv_depth + center_x
    image_y = focal_length * view_pos[1] * inv_depth + center_y
    scales = jnp.exp(params[3:6])
    local_axes = quat_rotation(params[6:10]) * scales[None, :, :]
    world_axes = jnp.einsum("ik,kjg->ijg", rotate, local_axes, precision=precise)
    proj_x = (
        focal_length * inv_depth * world_axes[0]
        - focal_length * view_pos[0] * inv_depth * inv_depth * world_axes[2]
    )
    proj_y = (
        focal_length * inv_depth * world_axes[1]
        - focal_length * view_pos[1] * inv_depth * inv_depth * world_axes[2]
    )
    cov_xx = jnp.sum(proj_x * proj_x, axis=0) + 0.3
    cov_xy = jnp.sum(proj_x * proj_y, axis=0)
    cov_yy = jnp.sum(proj_y * proj_y, axis=0) + 0.3
    determ = cov_xx * cov_yy - cov_xy * cov_xy
    opacity = 0.99 * jax.nn.sigmoid(params[10])
    center = -jnp.dot(rotate.T, shift, precision=precise)
    offset = means - center[:, None]
    direction = offset / jnp.sqrt(jnp.sum(offset * offset, axis=0))
    basis = sh_basis(direction)
    coeffs = params[11:59].reshape(16, 3, -1)
    colors = 0.5 + jnp.sum(basis[:, None, :] * coeffs, axis=0)
    head = jnp.stack(
        [image_x, image_y, cov_yy / determ, -cov_xy / determ, cov_xx / determ, opacity]
    )
    return jnp.concatenate([head, colors], axis=0)


def pixel_grid(tile, tile_cols):
    offsets = jnp.arange(PIXELS)
    pixel_x = (tile % tile_cols * TILE_SIDE + offsets % TILE_SIDE).astype(jnp.float32) + 0.5
    pixel_y = (tile // tile_cols * TILE_SIDE + offsets // TILE_SIDE).astype(jnp.float32) + 0.5
    return (pixel_x, pixel_y)


def block_terms(entry, count, pixel_x, pixel_y, index):
    start = index * BLOCK
    piece = lax.dynamic_slice_in_dim(entry, start, BLOCK, 1)
    live = (start + jnp.arange(BLOCK) < count)[None, :]
    delta_x = pixel_x[:, None] - piece[0][None, :]
    delta_y = pixel_y[:, None] - piece[1][None, :]
    power = -0.5 * (
        piece[2] * delta_x * delta_x
        + 2.0 * piece[3] * delta_x * delta_y
        + piece[4] * delta_y * delta_y
    )
    falloff = jnp.exp(power)
    alpha = jnp.where(live, piece[5][None, :] * falloff, 0.0)
    log_keep = jnp.log1p(-alpha)
    return (start, piece, live, delta_x, delta_y, falloff, alpha, log_keep)


def tile_pass(entry, count, pixel_x, pixel_y, target, background):
    blocks = (count + BLOCK - 1) // BLOCK

    def forward(index, carry):
        color, log_total = carry
        start, piece, live, delta_x, delta_y, falloff, alpha, log_keep = block_terms(
            entry, count, pixel_x, pixel_y, index
        )
        weight = jnp.exp(log_total[:, None] + jnp.cumsum(log_keep, axis=1) - log_keep) * alpha
        color = color + lax.dot_general(
            piece[6:9], weight, (((1,), (1,)), ((), ())), precision=precise
        )
        return (color, log_total + jnp.sum(log_keep, axis=1))

    zeros_pix = jnp.zeros((PIXELS,), jnp.float32)
    color, log_total = lax.fori_loop(
        0, blocks, forward, (jnp.zeros((3, PIXELS), jnp.float32), zeros_pix)
    )
    image = color + jnp.exp(log_total)[None, :] * background[:, None]
    resid = image - target
    dot_total = jnp.sum(image * resid, axis=0)

    def backward(index, carry):
        grads, log_before, prefix = carry
        start, piece, live, delta_x, delta_y, falloff, alpha, log_keep = block_terms(
            entry, count, pixel_x, pixel_y, index
        )
        trans = jnp.exp(log_before[:, None] + jnp.cumsum(log_keep, axis=1) - log_keep)
        weight = trans * alpha
        along = lax.dot_general(resid, piece[6:9], (((0,), (0,)), ((), ())), precision=precise)
        running = prefix[:, None] + jnp.cumsum(weight * along, axis=1)
        d_alpha = jnp.where(
            live, trans * along - (dot_total[:, None] - running) / (1.0 - alpha), 0.0
        )
        d_power = d_alpha * alpha
        sum_x = jnp.sum(d_power * delta_x, axis=0)
        sum_y = jnp.sum(d_power * delta_y, axis=0)
        head = jnp.stack(
            [
                piece[2] * sum_x + piece[3] * sum_y,
                piece[3] * sum_x + piece[4] * sum_y,
                -0.5 * jnp.sum(d_power * delta_x * delta_x, axis=0),
                -jnp.sum(d_power * delta_x * delta_y, axis=0),
                -0.5 * jnp.sum(d_power * delta_y * delta_y, axis=0),
                jnp.sum(d_alpha * falloff, axis=0),
            ]
        )
        color_grad = jnp.dot(resid, weight, precision=precise)
        block_grad = jnp.concatenate([head, color_grad], axis=0)
        grads = lax.dynamic_update_slice_in_dim(grads, block_grad, start, 1)
        return (grads, log_before + jnp.sum(log_keep, axis=1), running[:, -1])

    start_grads = jnp.zeros((9, LIST), jnp.float32)
    grads, ignored, unused = lax.fori_loop(0, blocks, backward, (start_grads, zeros_pix, zeros_pix))
    return (image, grads)


def split_cumsum(x, upper):
    high = x.astype(jnp.bfloat16)
    rest = x - high.astype(jnp.float32)
    middle = rest.astype(jnp.bfloat16)
    low = (rest - middle.astype(jnp.float32)).astype(jnp.bfloat16)
    total = jnp.dot(high, upper, preferred_element_type=jnp.float32)
    total = total + jnp.dot(middle, upper, preferred_element_type=jnp.float32)
    return total + jnp.dot(low, upper, preferred_element_type=jnp.float32)


def render_kernel(
    counts_ref, tiles_ref, entry_ref, target_ref, bg_ref, image_ref, sums_ref, trans_ref, fall_ref, *, tile_cols
):
    t = pl.program_id(0)
    count = counts_ref[t]
    tile = tiles_ref[t]
    blocks = (count + KB - 1) // KB
    sums_ref[...] = jnp.zeros(sums_ref.shape, jnp.float32)
    row = lax.broadcasted_iota(jnp.int32, (KB, KB), 0)
    col = lax.broadcasted_iota(jnp.int32, (KB, KB), 1)
    upper = (row <= col).astype(jnp.bfloat16)
    lane = lax.broadcasted_iota(jnp.int32, (1, KB), 1)
    pixel = lax.broadcasted_iota(jnp.int32, (PIXELS, KB), 0)
    pix_x = ((tile % tile_cols) * TILE_SIDE + pixel % TILE_SIDE).astype(jnp.float32) + 0.5
    pix_y = ((tile // tile_cols) * TILE_SIDE + pixel // TILE_SIDE).astype(jnp.float32) + 0.5

    def geometry(index):
        start = pl.multiple_of(index * KB, KB)
        blk = entry_ref[:, pl.ds(start, KB)]
        live = (start + lane) < count
        return start, blk, live, pix_x - blk[0:1], pix_y - blk[1:2]

    def forward(i, carry):
        log_total, red, green, blue = carry
        start, blk, live, dx, dy = geometry(i)
        power = -0.5 * (blk[2:3] * dx * dx + 2.0 * blk[3:4] * dx * dy + blk[4:5] * dy * dy)
        falloff = jnp.exp(power)
        alpha = jnp.where(live, blk[5:6] * falloff, 0.0)
        log_keep = jnp.log1p(-alpha)
        cum = split_cumsum(log_keep, upper)
        trans = jnp.exp(log_total + cum - log_keep)
        weight = trans * alpha
        trans_ref[:, pl.ds(start, KB)] = trans
        fall_ref[:, pl.ds(start, KB)] = falloff
        return (
            log_total + cum[:, KB - 1 : KB],
            red + weight * blk[8:9],
            green + weight * blk[9:10],
            blue + weight * blk[10:11],
        )

    zeros = jnp.zeros((PIXELS, KB), jnp.float32)
    log_total, red, green, blue = lax.fori_loop(
        0, blocks, forward, (jnp.zeros((PIXELS, 1), jnp.float32), zeros, zeros, zeros)
    )
    lane8 = lax.broadcasted_iota(jnp.int32, (1, 8), 1)
    color = (
        jnp.where(lane8 == 0, jnp.sum(red, axis=1, keepdims=True), 0.0)
        + jnp.where(lane8 == 1, jnp.sum(green, axis=1, keepdims=True), 0.0)
        + jnp.where(lane8 == 2, jnp.sum(blue, axis=1, keepdims=True), 0.0)
    )
    image = color + jnp.exp(log_total) * bg_ref[...]
    image_ref[...] = image
    resid = image - target_ref[...]
    dot_total = jnp.sum(image * resid, axis=1, keepdims=True)
    resid_r, resid_g, resid_b = resid[:, 0:1], resid[:, 1:2], resid[:, 2:3]

    def backward(i, prefix):
        start, blk, live, dx, dy = geometry(i)
        trans = trans_ref[:, pl.ds(start, KB)]
        falloff = fall_ref[:, pl.ds(start, KB)]
        alpha = jnp.where(live, blk[5:6] * falloff, 0.0)
        weight = trans * alpha
        along = resid_r * blk[8:9] + resid_g * blk[9:10] + resid_b * blk[10:11]
        running = prefix + split_cumsum(weight * along, upper)
        d_alpha = jnp.where(live, trans * along - (dot_total - running) / (1.0 - alpha), 0.0)
        d_power = d_alpha * alpha
        x_term = d_power * dx
        y_term = d_power * dy
        parts = [
            x_term,
            y_term,
            x_term * dx,
            x_term * dy,
            y_term * dy,
            d_alpha * falloff,
            weight * resid_r,
            weight * resid_g,
            weight * resid_b,
        ]
        for r, part in enumerate(parts):
            sums_ref[r : r + 1, pl.ds(start, KB)] += jnp.sum(part, axis=0, keepdims=True)
        return running[:, KB - 1 : KB]

    lax.fori_loop(0, blocks, backward, jnp.zeros((PIXELS, 1), jnp.float32))


def render_tiles(entry16, counts, tiles, target8, bg8, tile_cols):
    n = entry16.shape[0]
    return pl.pallas_call(
        partial(render_kernel, tile_cols=tile_cols),
        grid=(n,),
        in_specs=[
            pl.BlockSpec(memory_space=pltpu.SMEM),
            pl.BlockSpec(memory_space=pltpu.SMEM),
            pl.BlockSpec((None, 16, LIST), lambda t: (t, 0, 0)),
            pl.BlockSpec((None, PIXELS, 8), lambda t: (t, 0, 0)),
            pl.BlockSpec((1, 8), lambda t: (0, 0)),
        ],
        out_specs=[
            pl.BlockSpec((None, PIXELS, 8), lambda t: (t, 0, 0)),
            pl.BlockSpec((None, 16, LIST), lambda t: (t, 0, 0)),
        ],
        out_shape=[
            jax.ShapeDtypeStruct((n, PIXELS, 8), jnp.float32),
            jax.ShapeDtypeStruct((n, 16, LIST), jnp.float32),
        ],
        scratch_shapes=[
            pltpu.VMEM((PIXELS, LIST), jnp.float32),
            pltpu.VMEM((PIXELS, LIST), jnp.float32),
        ],
    )(counts, tiles, entry16, target8, bg8)


def select_rows(values, chosen, contract):
    high = lax.reduce_precision(values, exponent_bits=8, mantissa_bits=7)
    rest = values - high
    middle = lax.reduce_precision(rest, exponent_bits=8, mantissa_bits=7)
    low = rest - middle
    pieces = jnp.concatenate([high, middle, low], axis=0).astype(jnp.bfloat16)
    out = lax.dot_general(
        pieces, chosen, (((1,), (contract,)), ((), ())), preferred_element_type=jnp.float32
    )
    rows = values.shape[0]
    return (out[:rows] + out[rows : 2 * rows]) + out[2 * rows :]


def adam_step(values, first, second, grad, rates):
    first_new = decay_one * first + (1.0 - decay_one) * grad
    second_new = decay_two * second + (1.0 - decay_two) * grad * grad
    return (
        values - rates[:, None] * first_new / (jnp.sqrt(second_new) + adam_epsilon),
        first_new,
        second_new,
    )


def body(
    gaussians,
    moment_one,
    moment_two,
    learn_rates,
    cameras,
    camera_ids,
    list_owner,
    list_index,
    list_length,
    targets,
    background,
):
    peers = lax.axis_size("tiles")
    tiles_here = list_index.shape[1]
    entries = tiles_here * LIST
    owned = gaussians.shape[1]
    capacity = 2 * entries // peers
    tile_cols = tiles_here * peers // TILE_ROWS
    center_x = 0.5 * TILE_SIDE * tile_cols
    center_y = 0.5 * TILE_SIDE * TILE_ROWS
    camera = cameras[camera_ids[0]]
    attrs = project(gaussians, camera, center_x, center_y)
    owner_flat = list_owner.reshape(-1)
    index_flat = list_index.reshape(-1)
    earlier = jnp.arange(entries)[None, :] < jnp.arange(entries)[:, None]
    same = owner_flat[:, None] == owner_flat[None, :]
    rank = jnp.sum((same & earlier).astype(jnp.int32), axis=1)
    slot = owner_flat * capacity + rank
    placed = (slot[:, None] == jnp.arange(peers * capacity)[None, :]).astype(jnp.bfloat16)
    asked_for = (
        jnp.round(select_rows(index_flat.astype(jnp.float32)[None], placed, 0))
        .astype(jnp.int32)
        .reshape(peers, capacity)
    )
    asked = lax.all_to_all(asked_for, "tiles", split_axis=0, concat_axis=0, tiled=True)
    chosen = (asked.reshape(-1)[:, None] == jnp.arange(owned)[None, :]).astype(jnp.bfloat16)
    served = select_rows(attrs, chosen, 1).reshape(9, peers, capacity)
    returned = lax.all_to_all(served, "tiles", split_axis=1, concat_axis=1, tiled=True)
    entry_attrs = select_rows(returned.reshape(9, peers * capacity), placed, 1).reshape(
        9, tiles_here, LIST
    )
    first_tile = lax.axis_index("tiles") * tiles_here

    colors_pad = jnp.zeros((5, tiles_here, LIST), jnp.float32)
    entry16 = jnp.moveaxis(
        jnp.concatenate([entry_attrs[0:6], colors_pad[0:2], entry_attrs[6:9], colors_pad], axis=0), 1, 0
    )
    target8 = jnp.pad(
        jnp.swapaxes(targets[0].astype(jnp.float32), 1, 2), ((0, 0), (0, 0), (0, 5))
    )
    background8 = jnp.pad(background, (0, 5))[None]
    tile_ids = first_tile + jnp.arange(tiles_here, dtype=jnp.int32)
    image8, sums = render_tiles(entry16, list_length[0], tile_ids, target8, background8, tile_cols)
    images = jnp.swapaxes(image8[:, :, 0:3], 1, 2)
    sums = jnp.moveaxis(sums, 1, 0).reshape(16, entries)
    flat = entry_attrs.reshape(9, entries)
    flat_grads = jnp.stack(
        [
            flat[2] * sums[0] + flat[3] * sums[1],
            flat[3] * sums[0] + flat[4] * sums[1],
            -0.5 * sums[2],
            -sums[3],
            -0.5 * sums[4],
            sums[5],
            sums[6],
            sums[7],
            sums[8],
        ]
    )
    grad_send = select_rows(flat_grads, placed, 0).reshape(9, peers, capacity)
    grad_back = lax.all_to_all(grad_send, "tiles", split_axis=1, concat_axis=1, tiled=True)
    attr_grad = select_rows(grad_back.reshape(9, peers * capacity), chosen, 0)
    payload = jnp.concatenate([attr_grad.reshape(-1), jnp.pad(camera, (0, 128 - 12))])
    gathered = lax.all_gather(payload.reshape(-1, 128), "views", axis=0, tiled=False)
    gathered = gathered.reshape(gathered.shape[0], -1)
    view_grads = gathered[:, : 9 * owned].reshape(-1, 9, owned)
    view_cameras = gathered[:, 9 * owned : 9 * owned + 12]

    def pull(view_camera, grad):
        ignored, pullback = jax.vjp(
            partial(project, camera=view_camera, center_x=center_x, center_y=center_y),
            gaussians,
        )
        return pullback(grad)[0]

    total = jnp.sum(jax.vmap(pull)(view_cameras, view_grads), axis=0)
    new_values, first_new, second_new = adam_step(
        gaussians, moment_one, moment_two, total, learn_rates
    )
    return (images[None].astype(jnp.bfloat16), new_values, first_new, second_new)


def solution(mesh):
    return jax.shard_map(
        body,
        mesh=mesh,
        in_specs=(
            P(None, "tiles"),
            P(None, "tiles"),
            P(None, "tiles"),
            P(),
            P(),
            P("views"),
            P("views", "tiles", None, None),
            P("views", "tiles", None),
            P("views", "tiles"),
            P("views", "tiles", None, None),
            P(),
        ),
        out_specs=(
            P("views", "tiles", None, None),
            P(None, "tiles"),
            P(None, "tiles"),
            P(None, "tiles"),
        ),
        check_vma=False,
    )
```

```python
from functools import partial

import jax
import jax.numpy as jnp
from jax import lax
from jax.experimental import pallas as pl
from jax.experimental.pallas import tpu as pltpu
from jax.sharding import PartitionSpec as P

TILE_SIDE = 32
PIXELS = 1024
TILE_ROWS = 8
LIST = 1024
BLOCK = 128
KB = 256


focal_length = 400.0
precise = lax.Precision.HIGHEST
decay_one = 0.9
decay_two = 0.999
adam_epsilon = 1e-08


def sh_basis(direction):
    dir_x, dir_y, dir_z = (direction[0], direction[1], direction[2])
    sq_x, sq_y, sq_z = (dir_x * dir_x, dir_y * dir_y, dir_z * dir_z)
    terms = [
        0.28209479177387814 * jnp.ones_like(dir_x),
        -0.4886025119029199 * dir_y,
        0.4886025119029199 * dir_z,
        -0.4886025119029199 * dir_x,
        1.0925484305920792 * dir_x * dir_y,
        -1.0925484305920792 * dir_y * dir_z,
        0.31539156525252005 * (2.0 * sq_z - sq_x - sq_y),
        -1.0925484305920792 * dir_x * dir_z,
        0.5462742152960396 * (sq_x - sq_y),
        -0.5900435899266435 * dir_y * (3.0 * sq_x - sq_y),
        2.890611442640554 * dir_x * dir_y * dir_z,
        -0.4570457994644658 * dir_y * (4.0 * sq_z - sq_x - sq_y),
        0.3731763325901154 * dir_z * (2.0 * sq_z - 3.0 * sq_x - 3.0 * sq_y),
        -0.4570457994644658 * dir_x * (4.0 * sq_z - sq_x - sq_y),
        1.445305721320277 * dir_z * (sq_x - sq_y),
        -0.5900435899266435 * dir_x * (sq_x - 3.0 * sq_y),
    ]
    return jnp.stack(terms)


def quat_rotation(quat):
    length = jnp.sqrt(jnp.sum(quat * quat, axis=0))
    quat_w, quat_x, quat_y, quat_z = (
        quat[0] / length,
        quat[1] / length,
        quat[2] / length,
        quat[3] / length,
    )
    rows = [
        [
            1.0 - 2.0 * (quat_y * quat_y + quat_z * quat_z),
            2.0 * (quat_x * quat_y - quat_w * quat_z),
            2.0 * (quat_x * quat_z + quat_w * quat_y),
        ],
        [
            2.0 * (quat_x * quat_y + quat_w * quat_z),
            1.0 - 2.0 * (quat_x * quat_x + quat_z * quat_z),
            2.0 * (quat_y * quat_z - quat_w * quat_x),
        ],
        [
            2.0 * (quat_x * quat_z - quat_w * quat_y),
            2.0 * (quat_y * quat_z + quat_w * quat_x),
            1.0 - 2.0 * (quat_x * quat_x + quat_y * quat_y),
        ],
    ]
    return jnp.stack([jnp.stack(entries) for entries in rows])


def project(params, camera, center_x, center_y):
    means = params[0:3]
    rotate = camera[0:9].reshape(3, 3)
    shift = camera[9:12]
    view_pos = jnp.dot(rotate, means, precision=precise) + shift[:, None]
    inv_depth = 1.0 / view_pos[2]
    image_x = focal_length * view_pos[0] * inv_depth + center_x
    image_y = focal_length * view_pos[1] * inv_depth + center_y
    scales = jnp.exp(params[3:6])
    local_axes = quat_rotation(params[6:10]) * scales[None, :, :]
    world_axes = jnp.einsum("ik,kjg->ijg", rotate, local_axes, precision=precise)
    proj_x = (
        focal_length * inv_depth * world_axes[0]
        - focal_length * view_pos[0] * inv_depth * inv_depth * world_axes[2]
    )
    proj_y = (
        focal_length * inv_depth * world_axes[1]
        - focal_length * view_pos[1] * inv_depth * inv_depth * world_axes[2]
    )
    cov_xx = jnp.sum(proj_x * proj_x, axis=0) + 0.3
    cov_xy = jnp.sum(proj_x * proj_y, axis=0)
    cov_yy = jnp.sum(proj_y * proj_y, axis=0) + 0.3
    determ = cov_xx * cov_yy - cov_xy * cov_xy
    opacity = 0.99 * jax.nn.sigmoid(params[10])
    center = -jnp.dot(rotate.T, shift, precision=precise)
    offset = means - center[:, None]
    direction = offset / jnp.sqrt(jnp.sum(offset * offset, axis=0))
    basis = sh_basis(direction)
    coeffs = params[11:59].reshape(16, 3, -1)
    colors = 0.5 + jnp.sum(basis[:, None, :] * coeffs, axis=0)
    head = jnp.stack(
        [image_x, image_y, cov_yy / determ, -cov_xy / determ, cov_xx / determ, opacity]
    )
    return jnp.concatenate([head, colors], axis=0)


def pixel_grid(tile, tile_cols):
    offsets = jnp.arange(PIXELS)
    pixel_x = (tile % tile_cols * TILE_SIDE + offsets % TILE_SIDE).astype(jnp.float32) + 0.5
    pixel_y = (tile // tile_cols * TILE_SIDE + offsets // TILE_SIDE).astype(jnp.float32) + 0.5
    return (pixel_x, pixel_y)


def block_terms(entry, count, pixel_x, pixel_y, index):
    start = index * BLOCK
    piece = lax.dynamic_slice_in_dim(entry, start, BLOCK, 1)
    live = (start + jnp.arange(BLOCK) < count)[None, :]
    delta_x = pixel_x[:, None] - piece[0][None, :]
    delta_y = pixel_y[:, None] - piece[1][None, :]
    power = -0.5 * (
        piece[2] * delta_x * delta_x
        + 2.0 * piece[3] * delta_x * delta_y
        + piece[4] * delta_y * delta_y
    )
    falloff = jnp.exp(power)
    alpha = jnp.where(live, piece[5][None, :] * falloff, 0.0)
    log_keep = jnp.log1p(-alpha)
    return (start, piece, live, delta_x, delta_y, falloff, alpha, log_keep)


def tile_pass(entry, count, pixel_x, pixel_y, target, background):
    blocks = (count + BLOCK - 1) // BLOCK

    def forward(index, carry):
        color, log_total = carry
        start, piece, live, delta_x, delta_y, falloff, alpha, log_keep = block_terms(
            entry, count, pixel_x, pixel_y, index
        )
        weight = jnp.exp(log_total[:, None] + jnp.cumsum(log_keep, axis=1) - log_keep) * alpha
        color = color + lax.dot_general(
            piece[6:9], weight, (((1,), (1,)), ((), ())), precision=precise
        )
        return (color, log_total + jnp.sum(log_keep, axis=1))

    zeros_pix = jnp.zeros((PIXELS,), jnp.float32)
    color, log_total = lax.fori_loop(
        0, blocks, forward, (jnp.zeros((3, PIXELS), jnp.float32), zeros_pix)
    )
    image = color + jnp.exp(log_total)[None, :] * background[:, None]
    resid = image - target
    dot_total = jnp.sum(image * resid, axis=0)

    def backward(index, carry):
        grads, log_before, prefix = carry
        start, piece, live, delta_x, delta_y, falloff, alpha, log_keep = block_terms(
            entry, count, pixel_x, pixel_y, index
        )
        trans = jnp.exp(log_before[:, None] + jnp.cumsum(log_keep, axis=1) - log_keep)
        weight = trans * alpha
        along = lax.dot_general(resid, piece[6:9], (((0,), (0,)), ((), ())), precision=precise)
        running = prefix[:, None] + jnp.cumsum(weight * along, axis=1)
        d_alpha = jnp.where(
            live, trans * along - (dot_total[:, None] - running) / (1.0 - alpha), 0.0
        )
        d_power = d_alpha * alpha
        sum_x = jnp.sum(d_power * delta_x, axis=0)
        sum_y = jnp.sum(d_power * delta_y, axis=0)
        head = jnp.stack(
            [
                piece[2] * sum_x + piece[3] * sum_y,
                piece[3] * sum_x + piece[4] * sum_y,
                -0.5 * jnp.sum(d_power * delta_x * delta_x, axis=0),
                -jnp.sum(d_power * delta_x * delta_y, axis=0),
                -0.5 * jnp.sum(d_power * delta_y * delta_y, axis=0),
                jnp.sum(d_alpha * falloff, axis=0),
            ]
        )
        color_grad = jnp.dot(resid, weight, precision=precise)
        block_grad = jnp.concatenate([head, color_grad], axis=0)
        grads = lax.dynamic_update_slice_in_dim(grads, block_grad, start, 1)
        return (grads, log_before + jnp.sum(log_keep, axis=1), running[:, -1])

    start_grads = jnp.zeros((9, LIST), jnp.float32)
    grads, ignored, unused = lax.fori_loop(0, blocks, backward, (start_grads, zeros_pix, zeros_pix))
    return (image, grads)


def split_cumsum(x, upper):
    high = x.astype(jnp.bfloat16)
    rest = x - high.astype(jnp.float32)
    middle = rest.astype(jnp.bfloat16)
    low = (rest - middle.astype(jnp.float32)).astype(jnp.bfloat16)
    total = jnp.dot(high, upper, preferred_element_type=jnp.float32)
    total = total + jnp.dot(middle, upper, preferred_element_type=jnp.float32)
    return total + jnp.dot(low, upper, preferred_element_type=jnp.float32)


def render_kernel(
    counts_ref, tiles_ref, entry_ref, target_ref, bg_ref, image_ref, sums_ref, trans_ref, fall_ref, inv_ref, *, tile_cols
):
    t = pl.program_id(0)
    count = counts_ref[t]
    tile = tiles_ref[t]
    blocks = (count + KB - 1) // KB
    sums_ref[...] = jnp.zeros(sums_ref.shape, jnp.float32)
    row = lax.broadcasted_iota(jnp.int32, (KB, KB), 0)
    col = lax.broadcasted_iota(jnp.int32, (KB, KB), 1)
    upper = (row <= col).astype(jnp.bfloat16)
    lane = lax.broadcasted_iota(jnp.int32, (1, KB), 1)
    pixel = lax.broadcasted_iota(jnp.int32, (PIXELS, KB), 0)
    pix_x = ((tile % tile_cols) * TILE_SIDE + pixel % TILE_SIDE).astype(jnp.float32) + 0.5
    pix_y = ((tile // tile_cols) * TILE_SIDE + pixel // TILE_SIDE).astype(jnp.float32) + 0.5

    def geometry(index):
        start = pl.multiple_of(index * KB, KB)
        blk = entry_ref[:, pl.ds(start, KB)]
        live = (start + lane) < count
        return start, blk, live, pix_x - blk[0:1], pix_y - blk[1:2]

    def forward(i, carry):
        log_total, red, green, blue = carry
        start, blk, live, dx, dy = geometry(i)
        power = -0.5 * (blk[2:3] * dx * dx + 2.0 * blk[3:4] * dx * dy + blk[4:5] * dy * dy)
        falloff = jnp.exp(power)
        alpha = jnp.where(live, blk[5:6] * falloff, 0.0)
        log_keep = jnp.log(1.0 - alpha)
        cum = split_cumsum(log_keep, upper)
        trans = jnp.exp(log_total + cum - log_keep)
        weight = trans * alpha
        trans_ref[:, pl.ds(start, KB)] = trans
        fall_ref[:, pl.ds(start, KB)] = falloff
        inv_ref[:, pl.ds(start, KB)] = jnp.exp(-log_keep)
        return (
            log_total + cum[:, KB - 1 : KB],
            red + weight * blk[8:9],
            green + weight * blk[9:10],
            blue + weight * blk[10:11],
        )

    zeros = jnp.zeros((PIXELS, KB), jnp.float32)
    log_total, red, green, blue = lax.fori_loop(
        0, blocks, forward, (jnp.zeros((PIXELS, 1), jnp.float32), zeros, zeros, zeros)
    )
    lane8 = lax.broadcasted_iota(jnp.int32, (1, 8), 1)
    color = (
        jnp.where(lane8 == 0, jnp.sum(red, axis=1, keepdims=True), 0.0)
        + jnp.where(lane8 == 1, jnp.sum(green, axis=1, keepdims=True), 0.0)
        + jnp.where(lane8 == 2, jnp.sum(blue, axis=1, keepdims=True), 0.0)
    )
    image = color + jnp.exp(log_total) * bg_ref[...]
    image_ref[...] = image
    resid = image - target_ref[...]
    dot_total = jnp.sum(image * resid, axis=1, keepdims=True)
    resid_r, resid_g, resid_b = resid[:, 0:1], resid[:, 1:2], resid[:, 2:3]

    def backward(i, prefix):
        start, blk, live, dx, dy = geometry(i)
        trans = trans_ref[:, pl.ds(start, KB)]
        falloff = fall_ref[:, pl.ds(start, KB)]
        alpha = jnp.where(live, blk[5:6] * falloff, 0.0)
        weight = trans * alpha
        along = resid_r * blk[8:9] + resid_g * blk[9:10] + resid_b * blk[10:11]
        running = prefix + split_cumsum(weight * along, upper)
        d_alpha = jnp.where(live, trans * along - (dot_total - running) * inv_ref[:, pl.ds(start, KB)], 0.0)
        d_power = d_alpha * alpha
        x_term = d_power * dx
        y_term = d_power * dy
        parts = [
            x_term,
            y_term,
            x_term * dx,
            x_term * dy,
            y_term * dy,
            d_alpha * falloff,
            weight * resid_r,
            weight * resid_g,
            weight * resid_b,
        ]
        for r, part in enumerate(parts):
            sums_ref[r : r + 1, pl.ds(start, KB)] += jnp.sum(part, axis=0, keepdims=True)
        return running[:, KB - 1 : KB]

    lax.fori_loop(0, blocks, backward, jnp.zeros((PIXELS, 1), jnp.float32))


def render_tiles(entry16, counts, tiles, target8, bg8, tile_cols):
    n = entry16.shape[0]
    return pl.pallas_call(
        partial(render_kernel, tile_cols=tile_cols),
        grid=(n,),
        in_specs=[
            pl.BlockSpec(memory_space=pltpu.SMEM),
            pl.BlockSpec(memory_space=pltpu.SMEM),
            pl.BlockSpec((None, 16, LIST), lambda t: (t, 0, 0)),
            pl.BlockSpec((None, PIXELS, 8), lambda t: (t, 0, 0)),
            pl.BlockSpec((1, 8), lambda t: (0, 0)),
        ],
        out_specs=[
            pl.BlockSpec((None, PIXELS, 8), lambda t: (t, 0, 0)),
            pl.BlockSpec((None, 16, LIST), lambda t: (t, 0, 0)),
        ],
        out_shape=[
            jax.ShapeDtypeStruct((n, PIXELS, 8), jnp.float32),
            jax.ShapeDtypeStruct((n, 16, LIST), jnp.float32),
        ],
        scratch_shapes=[
            pltpu.VMEM((PIXELS, LIST), jnp.float32),
            pltpu.VMEM((PIXELS, LIST), jnp.float32),
            pltpu.VMEM((PIXELS, LIST), jnp.float32),
        ],
    )(counts, tiles, entry16, target8, bg8)


def select_rows(values, chosen, contract):
    high = lax.reduce_precision(values, exponent_bits=8, mantissa_bits=7)
    rest = values - high
    middle = lax.reduce_precision(rest, exponent_bits=8, mantissa_bits=7)
    low = rest - middle
    pieces = jnp.concatenate([high, middle, low], axis=0).astype(jnp.bfloat16)
    out = lax.dot_general(
        pieces, chosen, (((1,), (contract,)), ((), ())), preferred_element_type=jnp.float32
    )
    rows = values.shape[0]
    return (out[:rows] + out[rows : 2 * rows]) + out[2 * rows :]


def adam_step(values, first, second, grad, rates):
    first_new = decay_one * first + (1.0 - decay_one) * grad
    second_new = decay_two * second + (1.0 - decay_two) * grad * grad
    return (
        values - rates[:, None] * first_new / (jnp.sqrt(second_new) + adam_epsilon),
        first_new,
        second_new,
    )


def body(
    gaussians,
    moment_one,
    moment_two,
    learn_rates,
    cameras,
    camera_ids,
    list_owner,
    list_index,
    list_length,
    targets,
    background,
):
    peers = lax.axis_size("tiles")
    tiles_here = list_index.shape[1]
    entries = tiles_here * LIST
    owned = gaussians.shape[1]
    capacity = 2 * entries // peers
    tile_cols = tiles_here * peers // TILE_ROWS
    center_x = 0.5 * TILE_SIDE * tile_cols
    center_y = 0.5 * TILE_SIDE * TILE_ROWS
    camera = cameras[camera_ids[0]]
    attrs = project(gaussians, camera, center_x, center_y)
    owner_flat = list_owner.reshape(-1)
    index_flat = list_index.reshape(-1)
    earlier = jnp.arange(entries)[None, :] < jnp.arange(entries)[:, None]
    same = owner_flat[:, None] == owner_flat[None, :]
    rank = jnp.sum((same & earlier).astype(jnp.int32), axis=1)
    slot = owner_flat * capacity + rank
    placed = (slot[:, None] == jnp.arange(peers * capacity)[None, :]).astype(jnp.bfloat16)
    asked_for = (
        jnp.round(select_rows(index_flat.astype(jnp.float32)[None], placed, 0))
        .astype(jnp.int32)
        .reshape(peers, capacity)
    )
    asked = lax.all_to_all(asked_for, "tiles", split_axis=0, concat_axis=0, tiled=True)
    chosen = (asked.reshape(-1)[:, None] == jnp.arange(owned)[None, :]).astype(jnp.bfloat16)
    served = select_rows(attrs, chosen, 1).reshape(9, peers, capacity)
    returned = lax.all_to_all(served, "tiles", split_axis=1, concat_axis=1, tiled=True)
    entry_attrs = select_rows(returned.reshape(9, peers * capacity), placed, 1).reshape(
        9, tiles_here, LIST
    )
    first_tile = lax.axis_index("tiles") * tiles_here

    colors_pad = jnp.zeros((5, tiles_here, LIST), jnp.float32)
    entry16 = jnp.moveaxis(
        jnp.concatenate([entry_attrs[0:6], colors_pad[0:2], entry_attrs[6:9], colors_pad], axis=0), 1, 0
    )
    target8 = jnp.pad(
        jnp.swapaxes(targets[0].astype(jnp.float32), 1, 2), ((0, 0), (0, 0), (0, 5))
    )
    background8 = jnp.pad(background, (0, 5))[None]
    tile_ids = first_tile + jnp.arange(tiles_here, dtype=jnp.int32)
    image8, sums = render_tiles(entry16, list_length[0], tile_ids, target8, background8, tile_cols)
    images = jnp.swapaxes(image8[:, :, 0:3], 1, 2)
    sums = jnp.moveaxis(sums, 1, 0).reshape(16, entries)
    flat = entry_attrs.reshape(9, entries)
    flat_grads = jnp.stack(
        [
            flat[2] * sums[0] + flat[3] * sums[1],
            flat[3] * sums[0] + flat[4] * sums[1],
            -0.5 * sums[2],
            -sums[3],
            -0.5 * sums[4],
            sums[5],
            sums[6],
            sums[7],
            sums[8],
        ]
    )
    grad_send = select_rows(flat_grads, placed, 0).reshape(9, peers, capacity)
    grad_back = lax.all_to_all(grad_send, "tiles", split_axis=1, concat_axis=1, tiled=True)
    attr_grad = select_rows(grad_back.reshape(9, peers * capacity), chosen, 0)
    payload = jnp.concatenate([attr_grad.reshape(-1), jnp.pad(camera, (0, 128 - 12))])
    gathered = lax.all_gather(payload.reshape(-1, 128), "views", axis=0, tiled=False)
    gathered = gathered.reshape(gathered.shape[0], -1)
    view_grads = gathered[:, : 9 * owned].reshape(-1, 9, owned)
    view_cameras = gathered[:, 9 * owned : 9 * owned + 12]

    def pull(view_camera, grad):
        ignored, pullback = jax.vjp(
            partial(project, camera=view_camera, center_x=center_x, center_y=center_y),
            gaussians,
        )
        return pullback(grad)[0]

    total = jnp.sum(jax.vmap(pull)(view_cameras, view_grads), axis=0)
    new_values, first_new, second_new = adam_step(
        gaussians, moment_one, moment_two, total, learn_rates
    )
    return (images[None].astype(jnp.bfloat16), new_values, first_new, second_new)


def solution(mesh):
    return jax.shard_map(
        body,
        mesh=mesh,
        in_specs=(
            P(None, "tiles"),
            P(None, "tiles"),
            P(None, "tiles"),
            P(),
            P(),
            P("views"),
            P("views", "tiles", None, None),
            P("views", "tiles", None),
            P("views", "tiles"),
            P("views", "tiles", None, None),
            P(),
        ),
        out_specs=(
            P("views", "tiles", None, None),
            P(None, "tiles"),
            P(None, "tiles"),
            P(None, "tiles"),
        ),
        check_vma=False,
    )
```
